32 devices in a mesh: groups: 2 (over x), ctx: 8 (over z, y), heads: 2 (over core).
Axes of the slice: x: 2, y: 2, z: 4, core: 2. Of those that a mesh axis runs over, the one named last changes fastest.
Arguments:
- query_vectors: bfloat16 [2048, 16, 128], P(('groups', 'ctx'), 'heads'), parts along dimension 0, may hold values from -5.5 to 5.5
- key_vectors: bfloat16 [2048, 4, 128], P(('groups', 'ctx'), 'heads'), parts along dimension 0, may hold values from -5.5 to 5.5
- value_rows: bfloat16 [2048, 4, 128], P(('groups', 'ctx'), 'heads'), parts along dimension 0, may hold values from -6 to 6
- forward_out: bfloat16 [2048, 16, 128], P(('groups', 'ctx'), 'heads'), parts along dimension 0, may hold values from -3 to 3
- out_grad: bfloat16 [2048, 16, 128], P(('groups', 'ctx'), 'heads'), parts along dimension 0, may hold values from -24 to 24
- block_offsets: int32 [16], P(('groups', 'ctx')), parts along dimension 0, may hold values from 0 to 7, each once
Outputs:
- query_grad: float32 [2048, 16, 128], P(('groups', 'ctx'), 'heads'), parts along dimension 0
- key_gradient_array: float32 [2048, 4, 128], P(('groups', 'ctx'), 'heads'), parts along dimension 0
- value_gradient_array: float32 [2048, 4, 128], P(('groups', 'ctx'), 'heads'), parts along dimension 0
The draws below stay inside these ranges and needn't reach their ends.
There are 2 independent parts, one for each index of `groups`. The reference program is written for one: setup_inputs(seed, part) draws one part's arguments, and reference() takes and returns one part's arrays. A program takes and returns all parts, laid end to end along the dimension named above; each array names one. Nothing has to cross between parts.
Inputs may be any that keep to these rules, and one draw needn't show every extreme that they name: block_offsets is a permutation of 0 to 7.
All inputs are finite; a program needn't handle non-finite values.
Results may differ from the reference program's by a relative error of at most 0.0029.
Values may be sent and summed in bfloat16 or wider, within the bound.
No kernel may reach another device: no remote copies, remote signals or barrier semaphores. Data moves between devices by JAX's collectives and lax.ppermute only.
A program may use at most 64 MiB of HBM per device.

```python
import jax
import jax.numpy as jnp
from jax import lax

QUERY_HEADS = 16
KEY_VALUE_HEADS = 4
HEAD_SIZE = 128
TOK_DEV = 128
SEQUENCE_TOKENS = 1024
N_CTX = 8


def drawn_keys(key):
    starting_sample = jnp.clip(jax.random.normal(jax.random.fold_in(key, 11), (SEQUENCE_TOKENS, KEY_VALUE_HEADS, HEAD_SIZE), jnp.float32), -5.5, 5.5)
    return starting_sample


def draw_key_vectors(key, part):
    starting_sample = drawn_keys(key)
    result = starting_sample
    return result.astype(jnp.bfloat16)


def draw_query_vectors(key, part):
    starting_sample = jnp.clip(jax.random.normal(jax.random.fold_in(key, 21), (SEQUENCE_TOKENS, QUERY_HEADS, HEAD_SIZE), jnp.float32), -5.5, 5.5)
    result = starting_sample
    return result.astype(jnp.bfloat16)


def level_of(stream_key, extent, split, low, top_value):
    factor_of = 1.0
    for position, parts in split:
        heights = jax.random.uniform(jax.random.fold_in(jax.random.fold_in(stream_key, 6), position), (parts,), jnp.float32, low / len(split), top_value / len(split))
        factor_of = factor_of * jnp.repeat(jnp.exp(heights), extent[position] // parts).reshape((-1,) + (1,) * (len(extent) - 1 - position))
    return factor_of


def noise(rng, dims, width, bound, cuts=(), kind=jnp.bfloat16):
    drawn = jax.random.normal(rng, dims, jnp.float32) * width
    if len(cuts) > 0:
        drawn = level_of(rng, dims, cuts, -0.22, 0.18) * drawn
    return jnp.clip(drawn, min=-bound, max=bound).astype(kind)


def setup_inputs(seed: int = 0, part: int = 0) -> dict:
    seeds = jax.random.split(jax.random.key(seed), 7)
    part_keys = jax.random.split(jax.random.fold_in(seeds[6], part), 7)
    query_vectors = draw_query_vectors(jax.random.fold_in(jax.random.fold_in(seeds[6], part), 71), part)
    key_vectors = draw_key_vectors(jax.random.fold_in(jax.random.fold_in(seeds[6], part), 71), part)
    value_rows = noise(part_keys[2], (SEQUENCE_TOKENS, KEY_VALUE_HEADS, HEAD_SIZE), 1.0, 6.0, ((0, 8), (1, 2)))
    forward_out = noise(part_keys[3], (SEQUENCE_TOKENS, QUERY_HEADS, HEAD_SIZE), 0.5, 3.0, ((0, 8), (1, 2)))
    out_grad = noise(part_keys[4], (SEQUENCE_TOKENS, QUERY_HEADS, HEAD_SIZE), 4.0, 24.0, ((0, 8), (1, 2)))
    block_offsets = jax.random.permutation(part_keys[5], N_CTX).astype(jnp.int32)
    return {"query_vectors": query_vectors, "key_vectors": key_vectors, "value_rows": value_rows, "forward_out": forward_out, "out_grad": out_grad, "block_offsets": block_offsets}


def reference(query_vectors, key_vectors, value_rows, forward_out, out_grad, block_offsets):
    token_index = jnp.arange(SEQUENCE_TOKENS, dtype=jnp.int32)
    positions = block_offsets[token_index // TOK_DEV] * TOK_DEV + token_index % TOK_DEV
    visible = positions[None, :] <= positions[:, None]
    score_scale = HEAD_SIZE ** -0.5
    heads_per_group = QUERY_HEADS // KEY_VALUE_HEADS
    row_delta = jnp.sum(out_grad.astype(jnp.float32) * forward_out.astype(jnp.float32), axis=2)

    def one_head(head):
        kv_head = head // heads_per_group
        q_head = lax.dynamic_index_in_dim(query_vectors, head, 1, keepdims=False)
        g_head = lax.dynamic_index_in_dim(out_grad, head, 1, keepdims=False)
        k_head = lax.dynamic_index_in_dim(key_vectors, kv_head, 1, keepdims=False)
        v_head = lax.dynamic_index_in_dim(value_rows, kv_head, 1, keepdims=False)
        delta_head = lax.dynamic_index_in_dim(row_delta, head, 1, keepdims=False)
        scores = jnp.dot(q_head, k_head.T, preferred_element_type=jnp.float32) * score_scale
        scores = jnp.where(visible, scores, -1e30)
        row_max = jnp.max(scores, axis=1, keepdims=True)
        log_total = row_max + jnp.log(jnp.sum(jnp.exp(scores - row_max), axis=1, keepdims=True))
        probs = jnp.where(visible, jnp.exp(scores - log_total), 0.0)
        probs_low = probs.astype(jnp.bfloat16)
        prob_grad = jnp.dot(g_head, v_head.T, preferred_element_type=jnp.float32)
        score_grad = (probs * (prob_grad - delta_head[:, None])).astype(jnp.bfloat16)
        q_grad = jnp.dot(score_grad, k_head, preferred_element_type=jnp.float32) * score_scale
        k_grad = jnp.dot(score_grad.T, q_head, preferred_element_type=jnp.float32) * score_scale
        v_grad = jnp.dot(probs_low.T, g_head, preferred_element_type=jnp.float32)
        return q_grad, k_grad, v_grad

    q_grads, key_gradients, value_gradients = lax.map(one_head, jnp.arange(QUERY_HEADS, dtype=jnp.int32))
    query_grad = jnp.transpose(q_grads, (1, 0, 2))
    key_gradient_array = jnp.transpose(key_gradients.reshape(KEY_VALUE_HEADS, heads_per_group, SEQUENCE_TOKENS, HEAD_SIZE).sum(axis=1), (1, 0, 2))
    value_gradient_array = jnp.transpose(value_gradients.reshape(KEY_VALUE_HEADS, heads_per_group, SEQUENCE_TOKENS, HEAD_SIZE).sum(axis=1), (1, 0, 2))
    return query_grad, key_gradient_array, value_gradient_array
```

```python
import jax
import jax.numpy as jnp
from jax import lax
from jax.sharding import PartitionSpec as P

OFFSET_ROWS = 16


def on_device(query_vectors, key_vectors, value_rows, forward_out, out_grad, block_offsets):
    tok_rows, q_heads, head_width = query_vectors.shape
    kv_heads = key_vectors.shape[1]
    heads_per_group = q_heads // kv_heads
    cycle_size = lax.axis_size("ctx")
    score_scale = head_width ** (-0.5)
    kv_rows = tok_rows * kv_heads

    offset_rows = jnp.full((OFFSET_ROWS, head_width), block_offsets[0], jnp.float32).astype(jnp.bfloat16)
    slab = jnp.concatenate(
        [
            key_vectors.reshape(kv_rows, head_width),
            value_rows.reshape(kv_rows, head_width),
            offset_rows,
        ],
        axis=0,
    )
    gathered = lax.all_gather(slab, "ctx", axis=0, tiled=False)
    all_keys = gathered[:, :kv_rows].reshape(cycle_size * tok_rows, kv_heads, head_width)
    all_values = gathered[:, kv_rows : 2 * kv_rows].reshape(cycle_size * tok_rows, kv_heads, head_width)
    all_offsets = gathered[:, 2 * kv_rows, 0].astype(jnp.float32).astype(jnp.int32)

    row_index = jnp.arange(tok_rows, dtype=jnp.int32)
    key_positions = (all_offsets[:, None] * tok_rows + row_index[None, :]).reshape(-1)
    own_positions = block_offsets[0] * tok_rows + row_index
    visible = key_positions[None, :] <= own_positions[:, None]

    grouped_query = query_vectors.reshape(tok_rows, kv_heads, heads_per_group, head_width)
    grouped_grad = out_grad.reshape(tok_rows, kv_heads, heads_per_group, head_width)
    row_delta = jnp.sum(out_grad.astype(jnp.float32) * forward_out.astype(jnp.float32), axis=2)
    row_delta = row_delta.reshape(tok_rows, kv_heads, heads_per_group).transpose(1, 2, 0)

    scores = (
        jnp.einsum("tgrd,ugd->grtu", grouped_query, all_keys, preferred_element_type=jnp.float32)
        * score_scale
    )
    scores = jnp.where(visible, scores, -1e30)
    row_max = jnp.max(scores, axis=3, keepdims=True)
    log_total = row_max + jnp.log(jnp.sum(jnp.exp(scores - row_max), axis=3, keepdims=True))
    probs = jnp.where(visible, jnp.exp(scores - log_total), 0.0)
    probs_low = probs.astype(jnp.bfloat16)
    prob_grad = jnp.einsum(
        "tgrd,ugd->grtu", grouped_grad, all_values, preferred_element_type=jnp.float32
    )
    score_grad = (probs * (prob_grad - row_delta[..., None])).astype(jnp.bfloat16)
    query_grad = score_scale * jnp.einsum(
        "grtu,ugd->tgrd", score_grad, all_keys, preferred_element_type=jnp.float32
    )
    key_part = score_scale * jnp.einsum(
        "grtu,tgrd->ugd", score_grad, grouped_query, preferred_element_type=jnp.float32
    )
    value_part = jnp.einsum(
        "grtu,tgrd->ugd", probs_low, grouped_grad, preferred_element_type=jnp.float32
    )
    parts = jnp.concatenate([key_part, value_part], axis=1)
    owned = lax.psum_scatter(parts, "ctx", scatter_dimension=0, tiled=True)
    return (
        query_grad.reshape(tok_rows, q_heads, head_width),
        owned[:, :kv_heads],
        owned[:, kv_heads:],
    )


def solution(mesh):
    in_specs = (
        P(("groups", "ctx"), "heads", None),
        P(("groups", "ctx"), "heads", None),
        P(("groups", "ctx"), "heads", None),
        P(("groups", "ctx"), "heads", None),
        P(("groups", "ctx"), "heads", None),
        P(("groups", "ctx")),
    )
    out_specs = (
        P(("groups", "ctx"), "heads", None),
        P(("groups", "ctx"), "heads", None),
        P(("groups", "ctx"), "heads", None),
    )
    return jax.shard_map(
        on_device, mesh=mesh, in_specs=in_specs, out_specs=out_specs, check_vma=False
    )
```

```python
import jax
import jax.numpy as jnp
from jax import lax
from jax.sharding import PartitionSpec as P

OFFSET_ROWS = 16


def passed_along(value, axis, by):
    peers = lax.axis_size(axis)
    return lax.ppermute(value, axis, [(i, (i + by) % peers) for i in range(peers)])


def on_device(query_vectors, key_vectors, value_rows, forward_out, out_grad, block_offsets):
    tok_rows, q_heads, head_width = query_vectors.shape
    kv_heads = key_vectors.shape[1]
    heads_per_group = q_heads // kv_heads
    cycle_size = lax.axis_size("ctx")
    score_scale = head_width ** (-0.5)
    kv_rows = tok_rows * kv_heads

    offset_rows = jnp.full((OFFSET_ROWS, head_width), block_offsets[0], jnp.float32).astype(jnp.bfloat16)
    slab = jnp.concatenate(
        [
            key_vectors.reshape(kv_rows, head_width),
            value_rows.reshape(kv_rows, head_width),
            offset_rows,
        ],
        axis=0,
    )
    gathered = jnp.stack([slab] + [passed_along(slab, "ctx", s) for s in range(1, cycle_size)])
    all_keys = gathered[:, :kv_rows].reshape(cycle_size * tok_rows, kv_heads, head_width)
    all_values = gathered[:, kv_rows : 2 * kv_rows].reshape(cycle_size * tok_rows, kv_heads, head_width)
    all_offsets = gathered[:, 2 * kv_rows, 0].astype(jnp.float32).astype(jnp.int32)

    row_index = jnp.arange(tok_rows, dtype=jnp.int32)
    key_positions = (all_offsets[:, None] * tok_rows + row_index[None, :]).reshape(-1)
    own_positions = block_offsets[0] * tok_rows + row_index
    visible = key_positions[None, :] <= own_positions[:, None]

    grouped_query = query_vectors.reshape(tok_rows, kv_heads, heads_per_group, head_width)
    grouped_grad = out_grad.reshape(tok_rows, kv_heads, heads_per_group, head_width)
    row_delta = jnp.sum(out_grad.astype(jnp.float32) * forward_out.astype(jnp.float32), axis=2)
    row_delta = row_delta.reshape(tok_rows, kv_heads, heads_per_group).transpose(1, 2, 0)

    scores = (
        jnp.einsum("tgrd,ugd->grtu", grouped_query, all_keys, preferred_element_type=jnp.float32)
        * score_scale
    )
    scores = jnp.where(visible, scores, -1e30)
    row_max = jnp.max(scores, axis=3, keepdims=True)
    log_total = row_max + jnp.log(jnp.sum(jnp.exp(scores - row_max), axis=3, keepdims=True))
    probs = jnp.where(visible, jnp.exp(scores - log_total), 0.0)
    probs_low = probs.astype(jnp.bfloat16)
    prob_grad = jnp.einsum(
        "tgrd,ugd->grtu", grouped_grad, all_values, preferred_element_type=jnp.float32
    )
    score_grad = (probs * (prob_grad - row_delta[..., None])).astype(jnp.bfloat16)
    query_grad = score_scale * jnp.einsum(
        "grtu,ugd->tgrd", score_grad, all_keys, preferred_element_type=jnp.float32
    )
    key_part = score_scale * jnp.einsum(
        "grtu,tgrd->ugd", score_grad, grouped_query, preferred_element_type=jnp.float32
    )
    value_part = jnp.einsum(
        "grtu,tgrd->ugd", probs_low, grouped_grad, preferred_element_type=jnp.float32
    )
    parts = jnp.concatenate([key_part, value_part], axis=1).reshape(
        cycle_size, tok_rows, 2 * kv_heads, head_width
    )
    owned = parts[0]
    for s in range(1, cycle_size):
        owned = owned + passed_along(parts[s], "ctx", -s)
    return (
        query_grad.reshape(tok_rows, q_heads, head_width),
        owned[:, :kv_heads],
        owned[:, kv_heads:],
    )


def solution(mesh):
    in_specs = (
        P(("groups", "ctx"), "heads", None),
        P(("groups", "ctx"), "heads", None),
        P(("groups", "ctx"), "heads", None),
        P(("groups", "ctx"), "heads", None),
        P(("groups", "ctx"), "heads", None),
        P(("groups", "ctx")),
    )
    out_specs = (
        P(("groups", "ctx"), "heads", None),
        P(("groups", "ctx"), "heads", None),
        P(("groups", "ctx"), "heads", None),
    )
    return jax.shard_map(
        on_device, mesh=mesh, in_specs=in_specs, out_specs=out_specs, check_vma=False
    )
```

```python
import jax
import jax.numpy as jnp
from jax import lax
from jax.sharding import PartitionSpec as P

OFFSET_ROWS = 16


def passed_along(value, axis, by):
    peers = lax.axis_size(axis)
    return lax.ppermute(value, axis, [(i, (i + by) % peers) for i in range(peers)])


def on_device(query_vectors, key_vectors, value_rows, forward_out, out_grad, block_offsets):
    tok_rows, q_heads, head_width = query_vectors.shape
    kv_heads = key_vectors.shape[1]
    heads_per_group = q_heads // kv_heads
    cycle_size = lax.axis_size("ctx")
    score_scale = head_width ** (-0.5)
    kv_rows = tok_rows * kv_heads

    offset_rows = jnp.full((OFFSET_ROWS, head_width), block_offsets[0], jnp.float32).astype(jnp.bfloat16)
    slab = jnp.concatenate(
        [
            key_vectors.reshape(kv_rows, head_width),
            value_rows.reshape(kv_rows, head_width),
            offset_rows,
        ],
        axis=0,
    )
    gathered = jnp.stack([slab] + [passed_along(slab, "ctx", s) for s in range(1, cycle_size)])
    all_keys = gathered[:, :kv_rows].reshape(cycle_size * tok_rows, kv_heads, head_width)
    all_values = gathered[:, kv_rows : 2 * kv_rows].reshape(cycle_size * tok_rows, kv_heads, head_width)
    all_offsets = gathered[:, 2 * kv_rows, 0].astype(jnp.float32).astype(jnp.int32)

    row_index = jnp.arange(tok_rows, dtype=jnp.int32)
    key_positions = (all_offsets[:, None] * tok_rows + row_index[None, :]).reshape(-1)
    own_positions = block_offsets[0] * tok_rows + row_index
    visible = key_positions[None, :] <= own_positions[:, None]

    grouped_query = query_vectors.reshape(tok_rows, kv_heads, heads_per_group, head_width)
    grouped_grad = out_grad.reshape(tok_rows, kv_heads, heads_per_group, head_width)
    row_delta = jnp.sum(out_grad.astype(jnp.float32) * forward_out.astype(jnp.float32), axis=2)
    row_delta = row_delta.reshape(tok_rows, kv_heads, heads_per_group).transpose(1, 2, 0)

    scores = (
        jnp.einsum("tgrd,ugd->grtu", grouped_query, all_keys, preferred_element_type=jnp.float32)
        * score_scale
    )
    scores = jnp.where(visible, scores, -1e30)
    row_max = jnp.max(scores, axis=3, keepdims=True)
    log_total = row_max + jnp.log(jnp.sum(jnp.exp(scores - row_max), axis=3, keepdims=True))
    probs = jnp.where(visible, jnp.exp(scores - log_total), 0.0)
    probs_low = probs.astype(jnp.bfloat16)
    prob_grad = jnp.einsum(
        "tgrd,ugd->grtu", grouped_grad, all_values, preferred_element_type=jnp.float32
    )
    score_grad = (probs * (prob_grad - row_delta[..., None])).astype(jnp.bfloat16)
    query_grad = score_scale * jnp.einsum(
        "grtu,ugd->tgrd", score_grad, all_keys, preferred_element_type=jnp.float32
    )
    key_part = score_scale * jnp.einsum(
        "grtu,tgrd->ugd", score_grad, grouped_query, preferred_element_type=jnp.float32
    )
    value_part = jnp.einsum(
        "grtu,tgrd->ugd", probs_low, grouped_grad, preferred_element_type=jnp.float32
    )
    parts = jnp.concatenate([key_part, value_part], axis=1).reshape(
        cycle_size, tok_rows, 2 * kv_heads, head_width
    )
    owned = parts[0]
    for s in range(1, cycle_size):
        owned = owned + passed_along(parts[s].astype(jnp.bfloat16), "ctx", -s).astype(jnp.float32)
    return (
        query_grad.reshape(tok_rows, q_heads, head_width),
        owned[:, :kv_heads],
        owned[:, kv_heads:],
    )


def solution(mesh):
    in_specs = (
        P(("groups", "ctx"), "heads", None),
        P(("groups", "ctx"), "heads", None),
        P(("groups", "ctx"), "heads", None),
        P(("groups", "ctx"), "heads", None),
        P(("groups", "ctx"), "heads", None),
        P(("groups", "ctx")),
    )
    out_specs = (
        P(("groups", "ctx"), "heads", None),
        P(("groups", "ctx"), "heads", None),
        P(("groups", "ctx"), "heads", None),
    )
    return jax.shard_map(
        on_device, mesh=mesh, in_specs=in_specs, out_specs=out_specs, check_vma=False
    )
```

```python
import functools

import jax
import jax.numpy as jnp
from jax import lax
from jax.experimental import pallas as pl
from jax.experimental.pallas import tpu as pltpu
from jax.sharding import PartitionSpec as P

OFFSET_ROWS = 16
CHUNK_BLOCKS = 8
MASKED = -1e30


def passed_along(value, axis, by):
    peers = lax.axis_size(axis)
    return lax.ppermute(value, axis, [(i, (i + by) % peers) for i in range(peers)])


def backward_kernel(
    offs_ref, own_ref, q_ref, do_ref, fo_ref, kv_ref, dq_ref, own_part_ref, parts_ref,
    *, kv_heads, chunk_blocks
):
    q_heads, tok_rows, head_width = q_ref.shape
    blocks = kv_ref.shape[0]
    heads_per_group = q_heads // kv_heads
    rows = heads_per_group * tok_rows
    chunk_keys = chunk_blocks * tok_rows
    shift = tok_rows.bit_length() - 1
    scale = head_width ** (-0.5)
    f32 = jnp.float32
    row_pos = own_ref[0] * tok_rows + (
        lax.broadcasted_iota(jnp.int32, (rows, 1), 0) & (tok_rows - 1)
    )
    lane = lax.broadcasted_iota(jnp.int32, (1, chunk_keys), 1)
    lane_block = lax.shift_right_logical(lane, shift)
    lane_row = lane & (tok_rows - 1)

    def chunk_keys_of(c, g):
        k = kv_ref[c * chunk_blocks : (c + 1) * chunk_blocks, g * tok_rows : (g + 1) * tok_rows, :]
        return k.reshape(chunk_keys, head_width)

    def chunk_values_of(c, g):
        base = kv_heads * tok_rows + g * tok_rows
        v = kv_ref[c * chunk_blocks : (c + 1) * chunk_blocks, base : base + tok_rows, :]
        return v.reshape(chunk_keys, head_width)

    def chunk_scores(q, k, c):
        s = lax.dot_general(q, k, (((1,), (1,)), ((), ())), preferred_element_type=f32) * scale
        key_off = jnp.zeros((1, chunk_keys), jnp.int32)
        for b in range(chunk_blocks):
            key_off = jnp.where(lane_block == b, offs_ref[c * chunk_blocks + b], key_off)
        visible = (key_off * tok_rows + lane_row) <= row_pos
        return jnp.where(visible, s, MASKED), visible

    for g in range(kv_heads):
        heads = slice(g * heads_per_group, (g + 1) * heads_per_group)
        q = q_ref[heads].reshape(rows, head_width)
        do = do_ref[heads].reshape(rows, head_width)
        fo = fo_ref[heads].reshape(rows, head_width)
        delta = jnp.sum(do.astype(f32) * fo.astype(f32), axis=1, keepdims=True)

        run_max = jnp.full((rows, 1), MASKED, f32)
        run_total = jnp.zeros((rows, 1), f32)
        for c in range(blocks // chunk_blocks):
            s, _ = chunk_scores(q, chunk_keys_of(c, g), c)
            new_max = jnp.maximum(run_max, jnp.max(s, axis=1, keepdims=True))
            run_total = run_total * jnp.exp(run_max - new_max) + jnp.sum(
                jnp.exp(s - new_max), axis=1, keepdims=True
            )
            run_max = new_max
        log_total = run_max + jnp.log(run_total)

        dq = jnp.zeros((rows, head_width), f32)
        for c in range(blocks // chunk_blocks):
            k = chunk_keys_of(c, g)
            v = chunk_values_of(c, g)
            s, visible = chunk_scores(q, k, c)
            probs = jnp.where(visible, jnp.exp(s - log_total), 0.0)
            prob_grad = lax.dot_general(
                do, v, (((1,), (1,)), ((), ())), preferred_element_type=f32
            )
            score_grad = (probs * (prob_grad - delta)).astype(jnp.bfloat16)
            dq = dq + jnp.dot(score_grad, k, preferred_element_type=f32)
            dk = scale * lax.dot_general(
                score_grad, q, (((0,), (0,)), ((), ())), preferred_element_type=f32
            )
            dv = lax.dot_general(
                probs.astype(jnp.bfloat16), do, (((0,), (0,)), ((), ())), preferred_element_type=f32
            )
            for b in range(chunk_blocks):
                block = c * chunk_blocks + b
                piece = slice(b * tok_rows, (b + 1) * tok_rows)
                if block == 0:
                    own_part_ref[g] = dk[piece]
                    own_part_ref[kv_heads + g] = dv[piece]
                else:
                    parts_ref[block - 1, g] = dk[piece].astype(jnp.bfloat16)
                    parts_ref[block - 1, kv_heads + g] = dv[piece].astype(jnp.bfloat16)
        dq_ref[heads] = (scale * dq).reshape(heads_per_group, tok_rows, head_width)


def local_backward(offsets, own_offset, q_t, do_t, fo_t, gathered, kv_heads):
    q_heads, tok_rows, head_width = q_t.shape
    blocks = gathered.shape[0]
    chunk_blocks = min(CHUNK_BLOCKS, blocks)
    rows = q_heads * tok_rows
    keys = blocks * tok_rows
    smem = pl.BlockSpec(memory_space=pltpu.SMEM)
    vmem = pl.BlockSpec(memory_space=pltpu.VMEM)
    return pl.pallas_call(
        functools.partial(backward_kernel, kv_heads=kv_heads, chunk_blocks=chunk_blocks),
        out_shape=(
            jax.ShapeDtypeStruct((q_heads, tok_rows, head_width), jnp.float32),
            jax.ShapeDtypeStruct((2 * kv_heads, tok_rows, head_width), jnp.float32),
            jax.ShapeDtypeStruct((blocks - 1, 2 * kv_heads, tok_rows, head_width), jnp.bfloat16),
        ),
        in_specs=[smem, smem, vmem, vmem, vmem, vmem],
        out_specs=(vmem, vmem, vmem),
        compiler_params=pltpu.CompilerParams(vmem_limit_bytes=48 * 1024 * 1024),
        cost_estimate=pl.CostEstimate(
            flops=12 * rows * keys * head_width,
            transcendentals=2 * rows * keys,
            bytes_accessed=gathered.size * 2 + 3 * q_t.size * 2 + 6 * q_t.size,
        ),
    )(offsets, own_offset, q_t, do_t, fo_t, gathered)


def on_device(query_vectors, key_vectors, value_rows, forward_out, out_grad, block_offsets):
    tok_rows, q_heads, head_width = query_vectors.shape
    kv_heads = key_vectors.shape[1]
    cycle_size = lax.axis_size("ctx")
    kv_rows = tok_rows * kv_heads

    offset_rows = jnp.full((OFFSET_ROWS, head_width), block_offsets[0], jnp.float32).astype(jnp.bfloat16)
    slab = jnp.concatenate(
        [
            key_vectors.transpose(1, 0, 2).reshape(kv_rows, head_width),
            value_rows.transpose(1, 0, 2).reshape(kv_rows, head_width),
            offset_rows,
        ],
        axis=0,
    )
    gathered = jnp.stack([slab] + [passed_along(slab, "ctx", s) for s in range(1, cycle_size)])
    all_offsets = gathered[:, 2 * kv_rows, 0].astype(jnp.float32).astype(jnp.int32)

    dq_t, own_part, parts = local_backward(
        all_offsets,
        block_offsets,
        query_vectors.transpose(1, 0, 2),
        out_grad.transpose(1, 0, 2),
        forward_out.transpose(1, 0, 2),
        gathered,
        kv_heads,
    )
    arrived = [passed_along(parts[s - 1], "ctx", -s) for s in range(1, cycle_size)]
    key_grad = own_part[:kv_heads]
    value_grad = own_part[kv_heads:]
    for piece in arrived:
        key_grad = key_grad + piece[:kv_heads].astype(jnp.float32)
        value_grad = value_grad + piece[kv_heads:].astype(jnp.float32)
    return (
        dq_t.transpose(1, 0, 2),
        key_grad.transpose(1, 0, 2),
        value_grad.transpose(1, 0, 2),
    )


def solution(mesh):
    in_specs = (
        P(("groups", "ctx"), "heads", None),
        P(("groups", "ctx"), "heads", None),
        P(("groups", "ctx"), "heads", None),
        P(("groups", "ctx"), "heads", None),
        P(("groups", "ctx"), "heads", None),
        P(("groups", "ctx")),
    )
    out_specs = (
        P(("groups", "ctx"), "heads", None),
        P(("groups", "ctx"), "heads", None),
        P(("groups", "ctx"), "heads", None),
    )
    return jax.shard_map(
        on_device, mesh=mesh, in_specs=in_specs, out_specs=out_specs, check_vma=False
    )
```

```python
import functools

import jax
import jax.numpy as jnp
from jax import lax
from jax.experimental import pallas as pl
from jax.experimental.pallas import tpu as pltpu
from jax.sharding import PartitionSpec as P

OFFSET_ROWS = 16
CHUNK_BLOCKS = 8
MASKED = -1e30


def passed_along(value, axis, by):
    peers = lax.axis_size(axis)
    return lax.ppermute(value, axis, [(i, (i + by) % peers) for i in range(peers)])


def backward_kernel(
    offs_ref, own_ref, q_ref, do_ref, fo_ref, kv_ref, dq_ref, own_part_ref, parts_ref,
    *, kv_heads, chunk_blocks
):
    q_heads, tok_rows, head_width = q_ref.shape
    blocks = kv_ref.shape[0]
    heads_per_group = q_heads // kv_heads
    rows = heads_per_group * tok_rows
    chunk_keys = chunk_blocks * tok_rows
    shift = tok_rows.bit_length() - 1
    scale = head_width ** (-0.5)
    f32 = jnp.float32
    row_pos = own_ref[0] * tok_rows + (
        lax.broadcasted_iota(jnp.int32, (rows, 1), 0) & (tok_rows - 1)
    )
    lane = lax.broadcasted_iota(jnp.int32, (1, chunk_keys), 1)
    lane_block = lax.shift_right_logical(lane, shift)
    lane_row = lane & (tok_rows - 1)

    def chunk_keys_of(c, g):
        k = kv_ref[c * chunk_blocks : (c + 1) * chunk_blocks, g * tok_rows : (g + 1) * tok_rows, :]
        return k.reshape(chunk_keys, head_width)

    def chunk_values_of(c, g):
        base = kv_heads * tok_rows + g * tok_rows
        v = kv_ref[c * chunk_blocks : (c + 1) * chunk_blocks, base : base + tok_rows, :]
        return v.reshape(chunk_keys, head_width)

    def chunk_scores(q, k, c):
        s = lax.dot_general(q, k, (((1,), (1,)), ((), ())), preferred_element_type=f32) * scale
        key_off = jnp.zeros((1, chunk_keys), jnp.int32)
        for b in range(chunk_blocks):
            key_off = jnp.where(lane_block == b, offs_ref[c * chunk_blocks + b], key_off)
        visible = (key_off * tok_rows + lane_row) <= row_pos
        return jnp.where(visible, s, MASKED), visible

    for g in range(kv_heads):
        heads = slice(g * heads_per_group, (g + 1) * heads_per_group)
        q = q_ref[heads].reshape(rows, head_width)
        do = do_ref[heads].reshape(rows, head_width)
        fo = fo_ref[heads].reshape(rows, head_width)
        delta = jnp.sum(do.astype(f32) * fo.astype(f32), axis=1, keepdims=True)

        run_max = jnp.full((rows, 1), MASKED, f32)
        run_total = jnp.zeros((rows, 1), f32)
        for c in range(blocks // chunk_blocks):
            s, _ = chunk_scores(q, chunk_keys_of(c, g), c)
            new_max = jnp.maximum(run_max, jnp.max(s, axis=1, keepdims=True))
            run_total = run_total * jnp.exp(run_max - new_max) + jnp.sum(
                jnp.exp(s - new_max), axis=1, keepdims=True
            )
            run_max = new_max
        log_total = run_max + jnp.log(run_total)

        dq = jnp.zeros((rows, head_width), f32)
        for c in range(blocks // chunk_blocks):
            k = chunk_keys_of(c, g)
            v = chunk_values_of(c, g)
            s, visible = chunk_scores(q, k, c)
            probs = jnp.where(visible, jnp.exp(s - log_total), 0.0)
            prob_grad = lax.dot_general(
                do, v, (((1,), (1,)), ((), ())), preferred_element_type=f32
            )
            score_grad = (probs * (prob_grad - delta)).astype(jnp.bfloat16)
            dq = dq + jnp.dot(score_grad, k, preferred_element_type=f32)
            dk = scale * lax.dot_general(
                score_grad, q, (((0,), (0,)), ((), ())), preferred_element_type=f32
            )
            dv = lax.dot_general(
                probs.astype(jnp.bfloat16), do, (((0,), (0,)), ((), ())), preferred_element_type=f32
            )
            for b in range(chunk_blocks):
                block = c * chunk_blocks + b
                piece = slice(b * tok_rows, (b + 1) * tok_rows)
                if block == 0:
                    own_part_ref[g] = dk[piece]
                    own_part_ref[kv_heads + g] = dv[piece]
                else:
                    parts_ref[block - 1, g] = dk[piece].astype(jnp.bfloat16)
                    parts_ref[block - 1, kv_heads + g] = dv[piece].astype(jnp.bfloat16)
        dq_ref[heads] = (scale * dq).reshape(heads_per_group, tok_rows, head_width)


def local_backward(offsets, own_offset, q_t, do_t, fo_t, gathered, kv_heads):
    q_heads, tok_rows, head_width = q_t.shape
    blocks = gathered.shape[0]
    chunk_blocks = min(CHUNK_BLOCKS, blocks)
    rows = q_heads * tok_rows
    keys = blocks * tok_rows
    smem = pl.BlockSpec(memory_space=pltpu.SMEM)
    vmem = pl.BlockSpec(memory_space=pltpu.VMEM)
    return pl.pallas_call(
        functools.partial(backward_kernel, kv_heads=kv_heads, chunk_blocks=chunk_blocks),
        out_shape=(
            jax.ShapeDtypeStruct((q_heads, tok_rows, head_width), jnp.float32),
            jax.ShapeDtypeStruct((2 * kv_heads, tok_rows, head_width), jnp.float32),
            jax.ShapeDtypeStruct((blocks - 1, 2 * kv_heads, tok_rows, head_width), jnp.bfloat16),
        ),
        in_specs=[smem, smem, vmem, vmem, vmem, vmem],
        out_specs=(vmem, vmem, vmem),
        compiler_params=pltpu.CompilerParams(vmem_limit_bytes=48 * 1024 * 1024),
        cost_estimate=pl.CostEstimate(
            flops=12 * rows * keys * head_width,
            transcendentals=2 * rows * keys,
            bytes_accessed=gathered.size * 2 + 3 * q_t.size * 2 + 6 * q_t.size,
        ),
    )(offsets, own_offset, q_t, do_t, fo_t, gathered)


def on_device(query_vectors, key_vectors, value_rows, forward_out, out_grad, block_offsets):
    tok_rows, q_heads, head_width = query_vectors.shape
    kv_heads = key_vectors.shape[1]
    cycle_size = lax.axis_size("ctx")
    kv_rows = tok_rows * kv_heads

    offset_rows = jnp.full((OFFSET_ROWS, head_width), block_offsets[0], jnp.float32).astype(jnp.bfloat16)
    slab = jnp.concatenate(
        [
            key_vectors.transpose(1, 0, 2).reshape(kv_rows, head_width),
            value_rows.transpose(1, 0, 2).reshape(kv_rows, head_width),
            offset_rows,
        ],
        axis=0,
    )
    gathered = jnp.stack([slab] + [passed_along(slab, "ctx", s) for s in range(1, cycle_size)])
    all_offsets = gathered[:, 2 * kv_rows, 0].astype(jnp.float32).astype(jnp.int32)

    dq_t, own_part, parts = local_backward(
        all_offsets,
        block_offsets,
        query_vectors.transpose(1, 0, 2),
        out_grad.transpose(1, 0, 2),
        forward_out.transpose(1, 0, 2),
        gathered,
        kv_heads,
    )
    me = lax.axis_index("ctx")
    outgoing = jnp.concatenate([jnp.zeros_like(parts[:1]), parts], axis=0)
    outgoing = jnp.take(outgoing, (me - jnp.arange(cycle_size)) % cycle_size, axis=0)
    arrived = lax.all_to_all(outgoing, "ctx", 0, 0, tiled=True).astype(jnp.float32)
    key_grad = own_part[:kv_heads] + jnp.sum(arrived[:, :kv_heads], axis=0)
    value_grad = own_part[kv_heads:] + jnp.sum(arrived[:, kv_heads:], axis=0)
    return (
        dq_t.transpose(1, 0, 2),
        key_grad.transpose(1, 0, 2),
        value_grad.transpose(1, 0, 2),
    )


def solution(mesh):
    in_specs = (
        P(("groups", "ctx"), "heads", None),
        P(("groups", "ctx"), "heads", None),
        P(("groups", "ctx"), "heads", None),
        P(("groups", "ctx"), "heads", None),
        P(("groups", "ctx"), "heads", None),
        P(("groups", "ctx")),
    )
    out_specs = (
        P(("groups", "ctx"), "heads", None),
        P(("groups", "ctx"), "heads", None),
        P(("groups", "ctx"), "heads", None),
    )
    return jax.shard_map(
        on_device, mesh=mesh, in_specs=in_specs, out_specs=out_specs, check_vma=False
    )
```

```python
import functools

import jax
import jax.numpy as jnp
from jax import lax
from jax.experimental import pallas as pl
from jax.experimental.pallas import tpu as pltpu
from jax.sharding import PartitionSpec as P

OFFSET_ROWS = 16
CHUNK_BLOCKS = 8
MASKED = -1e30


def mate_pairs(peers, by):
    half = peers // 2
    return [(i, half * (i // half) + (i % half + by) % half) for i in range(peers)]


def mirror_pairs(peers):
    return [(i, (i + peers // 2) % peers) for i in range(peers)]


def backward_kernel(
    offs_ref, own_ref, q_ref, do_ref, fo_ref, kv_ref, dq_ref, own_part_ref, mirror_part_ref,
    parts_ref, *, kv_heads, chunk_blocks
):
    q_heads, tok_rows, head_width = q_ref.shape
    blocks = kv_ref.shape[0]
    heads_per_group = q_heads // kv_heads
    rows = heads_per_group * tok_rows
    chunk_keys = chunk_blocks * tok_rows
    shift = tok_rows.bit_length() - 1
    scale = head_width ** (-0.5)
    f32 = jnp.float32
    row_pos = own_ref[0] * tok_rows + (
        lax.broadcasted_iota(jnp.int32, (rows, 1), 0) & (tok_rows - 1)
    )
    lane = lax.broadcasted_iota(jnp.int32, (1, chunk_keys), 1)
    lane_block = lax.shift_right_logical(lane, shift)
    lane_row = lane & (tok_rows - 1)

    def chunk_keys_of(c, g):
        k = kv_ref[c * chunk_blocks : (c + 1) * chunk_blocks, g * tok_rows : (g + 1) * tok_rows, :]
        return k.reshape(chunk_keys, head_width)

    def chunk_values_of(c, g):
        base = kv_heads * tok_rows + g * tok_rows
        v = kv_ref[c * chunk_blocks : (c + 1) * chunk_blocks, base : base + tok_rows, :]
        return v.reshape(chunk_keys, head_width)

    def chunk_scores(q, k, c):
        s = lax.dot_general(q, k, (((1,), (1,)), ((), ())), preferred_element_type=f32) * scale
        key_off = jnp.zeros((1, chunk_keys), jnp.int32)
        for b in range(chunk_blocks):
            key_off = jnp.where(lane_block == b, offs_ref[c * chunk_blocks + b], key_off)
        visible = (key_off * tok_rows + lane_row) <= row_pos
        return jnp.where(visible, s, MASKED), visible

    for g in range(kv_heads):
        heads = slice(g * heads_per_group, (g + 1) * heads_per_group)
        q = q_ref[heads].reshape(rows, head_width)
        do = do_ref[heads].reshape(rows, head_width)
        fo = fo_ref[heads].reshape(rows, head_width)
        delta = jnp.sum(do.astype(f32) * fo.astype(f32), axis=1, keepdims=True)

        run_max = jnp.full((rows, 1), MASKED, f32)
        run_total = jnp.zeros((rows, 1), f32)
        for c in range(blocks // chunk_blocks):
            s, _ = chunk_scores(q, chunk_keys_of(c, g), c)
            new_max = jnp.maximum(run_max, jnp.max(s, axis=1, keepdims=True))
            run_total = run_total * jnp.exp(run_max - new_max) + jnp.sum(
                jnp.exp(s - new_max), axis=1, keepdims=True
            )
            run_max = new_max
        log_total = run_max + jnp.log(run_total)

        dq = jnp.zeros((rows, head_width), f32)
        for c in range(blocks // chunk_blocks):
            k = chunk_keys_of(c, g)
            v = chunk_values_of(c, g)
            s, visible = chunk_scores(q, k, c)
            probs = jnp.where(visible, jnp.exp(s - log_total), 0.0)
            prob_grad = lax.dot_general(
                do, v, (((1,), (1,)), ((), ())), preferred_element_type=f32
            )
            score_grad = (probs * (prob_grad - delta)).astype(jnp.bfloat16)
            dq = dq + jnp.dot(score_grad, k, preferred_element_type=f32)
            dk = scale * lax.dot_general(
                score_grad, q, (((0,), (0,)), ((), ())), preferred_element_type=f32
            )
            dv = lax.dot_general(
                probs.astype(jnp.bfloat16), do, (((0,), (0,)), ((), ())), preferred_element_type=f32
            )
            for b in range(chunk_blocks):
                block = c * chunk_blocks + b
                piece = slice(b * tok_rows, (b + 1) * tok_rows)
                if block == 0:
                    own_part_ref[g] = dk[piece]
                    own_part_ref[kv_heads + g] = dv[piece]
                else:
                    parts_ref[block - 1, g] = dk[piece].astype(jnp.bfloat16)
                    parts_ref[block - 1, kv_heads + g] = dv[piece].astype(jnp.bfloat16)
                if block == blocks // 2:
                    mirror_part_ref[g] = dk[piece]
                    mirror_part_ref[kv_heads + g] = dv[piece]
        dq_ref[heads] = (scale * dq).reshape(heads_per_group, tok_rows, head_width)


def local_backward(offsets, own_offset, q_t, do_t, fo_t, gathered, kv_heads):
    q_heads, tok_rows, head_width = q_t.shape
    blocks = gathered.shape[0]
    chunk_blocks = min(CHUNK_BLOCKS, blocks)
    rows = q_heads * tok_rows
    keys = blocks * tok_rows
    smem = pl.BlockSpec(memory_space=pltpu.SMEM)
    vmem = pl.BlockSpec(memory_space=pltpu.VMEM)
    return pl.pallas_call(
        functools.partial(backward_kernel, kv_heads=kv_heads, chunk_blocks=chunk_blocks),
        out_shape=(
            jax.ShapeDtypeStruct((q_heads, tok_rows, head_width), jnp.float32),
            jax.ShapeDtypeStruct((2 * kv_heads, tok_rows, head_width), jnp.float32),
            jax.ShapeDtypeStruct((2 * kv_heads, tok_rows, head_width), jnp.float32),
            jax.ShapeDtypeStruct((blocks - 1, 2 * kv_heads, tok_rows, head_width), jnp.bfloat16),
        ),
        in_specs=[smem, smem, vmem, vmem, vmem, vmem],
        out_specs=(vmem, vmem, vmem, vmem),
        compiler_params=pltpu.CompilerParams(vmem_limit_bytes=48 * 1024 * 1024),
        cost_estimate=pl.CostEstimate(
            flops=12 * rows * keys * head_width,
            transcendentals=2 * rows * keys,
            bytes_accessed=gathered.size * 2 + 3 * q_t.size * 2 + 6 * q_t.size,
        ),
    )(offsets, own_offset, q_t, do_t, fo_t, gathered)


def on_device(query_vectors, key_vectors, value_rows, forward_out, out_grad, block_offsets):
    tok_rows, q_heads, head_width = query_vectors.shape
    kv_heads = key_vectors.shape[1]
    cycle_size = lax.axis_size("ctx")
    kv_rows = tok_rows * kv_heads

    offset_rows = jnp.full((OFFSET_ROWS, head_width), block_offsets[0], jnp.float32).astype(jnp.bfloat16)
    paired = jnp.concatenate([key_vectors, value_rows], axis=1).transpose(1, 0, 2)
    slab = jnp.concatenate([paired.reshape(2 * kv_rows, head_width), offset_rows], axis=0)
    half = cycle_size // 2
    from_mates = [lax.ppermute(slab, "ctx", mate_pairs(cycle_size, k)) for k in range(1, half)]
    from_mirror = lax.ppermute(slab, "ctx", mirror_pairs(cycle_size))
    handed_on = [
        lax.ppermute(from_mirror, "ctx", mate_pairs(cycle_size, k)) for k in range(1, half)
    ]
    gathered = jnp.stack([slab] + from_mates + [from_mirror] + handed_on)
    all_offsets = gathered[:, 2 * kv_rows, 0].astype(jnp.float32).astype(jnp.int32)

    dq_t, own_part, mirror_part, parts = local_backward(
        all_offsets,
        block_offsets,
        query_vectors.transpose(1, 0, 2),
        out_grad.transpose(1, 0, 2),
        forward_out.transpose(1, 0, 2),
        gathered,
        kv_heads,
    )
    own_total = own_part
    mirror_total = mirror_part
    for k in range(1, half):
        pair = jnp.stack([parts[k - 1], parts[half + k - 1]])
        arrived = lax.ppermute(pair, "ctx", mate_pairs(cycle_size, half - k)).astype(jnp.float32)
        own_total = own_total + arrived[0]
        mirror_total = mirror_total + arrived[1]
    crossed = lax.ppermute(mirror_total.astype(jnp.bfloat16), "ctx", mirror_pairs(cycle_size))
    total = own_total + crossed.astype(jnp.float32)
    key_grad = total[:kv_heads].transpose(1, 0, 2)
    value_grad = total[kv_heads:].transpose(1, 0, 2)
    return (dq_t.transpose(1, 0, 2), key_grad, value_grad)


def solution(mesh):
    in_specs = (
        P(("groups", "ctx"), "heads", None),
        P(("groups", "ctx"), "heads", None),
        P(("groups", "ctx"), "heads", None),
        P(("groups", "ctx"), "heads", None),
        P(("groups", "ctx"), "heads", None),
        P(("groups", "ctx")),
    )
    out_specs = (
        P(("groups", "ctx"), "heads", None),
        P(("groups", "ctx"), "heads", None),
        P(("groups", "ctx"), "heads", None),
    )
    return jax.shard_map(
        on_device, mesh=mesh, in_specs=in_specs, out_specs=out_specs, check_vma=False
    )
```

```python
import functools

import jax
import jax.numpy as jnp
from jax import lax
from jax.experimental import pallas as pl
from jax.experimental.pallas import tpu as pltpu
from jax.sharding import PartitionSpec as P

OFFSET_ROWS = 16
CHUNK_BLOCKS = 8
MASKED = -1e30


def mate_pairs(peers, by):
    half = peers // 2
    return [(i, half * (i // half) + (i % half + by) % half) for i in range(peers)]


def mirror_pairs(peers):
    return [(i, (i + peers // 2) % peers) for i in range(peers)]


def backward_kernel(
    offs_ref, own_ref, q_ref, do_ref, fo_ref, kv_ref, dq_ref, own_part_ref, mirror_part_ref,
    parts_ref, *, kv_heads, chunk_blocks
):
    q_heads, tok_rows, head_width = q_ref.shape
    blocks = kv_ref.shape[0]
    heads_per_group = q_heads // kv_heads
    rows = heads_per_group * tok_rows
    chunk_keys = chunk_blocks * tok_rows
    shift = tok_rows.bit_length() - 1
    scale = head_width ** (-0.5)
    f32 = jnp.float32
    row_pos = own_ref[0] * tok_rows + (
        lax.broadcasted_iota(jnp.int32, (rows, 1), 0) & (tok_rows - 1)
    )
    lane = lax.broadcasted_iota(jnp.int32, (1, chunk_keys), 1)
    lane_block = lax.shift_right_logical(lane, shift)
    lane_row = lane & (tok_rows - 1)

    def chunk_keys_of(c, g):
        k = kv_ref[c * chunk_blocks : (c + 1) * chunk_blocks, g * tok_rows : (g + 1) * tok_rows, :]
        return k.reshape(chunk_keys, head_width)

    def chunk_values_of(c, g):
        base = kv_heads * tok_rows + g * tok_rows
        v = kv_ref[c * chunk_blocks : (c + 1) * chunk_blocks, base : base + tok_rows, :]
        return v.reshape(chunk_keys, head_width)

    def chunk_scores(q, k, c):
        s = lax.dot_general(q, k, (((1,), (1,)), ((), ())), preferred_element_type=f32) * scale
        key_off = jnp.zeros((1, chunk_keys), jnp.int32)
        for b in range(chunk_blocks):
            key_off = jnp.where(lane_block == b, offs_ref[c * chunk_blocks + b], key_off)
        visible = (key_off * tok_rows + lane_row) <= row_pos
        return jnp.where(visible, s, MASKED), visible

    for g in range(kv_heads):
        heads = slice(g * heads_per_group, (g + 1) * heads_per_group)
        q = q_ref[heads].reshape(rows, head_width)
        do = do_ref[heads].reshape(rows, head_width)
        fo = fo_ref[heads].reshape(rows, head_width)
        delta = jnp.sum(do.astype(f32) * fo.astype(f32), axis=1, keepdims=True)

        run_max = jnp.full((rows, 1), MASKED, f32)
        run_total = jnp.zeros((rows, 1), f32)
        for c in range(blocks // chunk_blocks):
            s, _ = chunk_scores(q, chunk_keys_of(c, g), c)
            new_max = jnp.maximum(run_max, jnp.max(s, axis=1, keepdims=True))
            run_total = run_total * jnp.exp(run_max - new_max) + jnp.sum(
                jnp.exp(s - new_max), axis=1, keepdims=True
            )
            run_max = new_max
        log_total = run_max + jnp.log(run_total)

        dq = jnp.zeros((rows, head_width), f32)
        for c in range(blocks // chunk_blocks):
            k = chunk_keys_of(c, g)
            v = chunk_values_of(c, g)
            s, visible = chunk_scores(q, k, c)
            probs = jnp.where(visible, jnp.exp(s - log_total), 0.0)
            prob_grad = lax.dot_general(
                do, v, (((1,), (1,)), ((), ())), preferred_element_type=f32
            )
            score_grad = (probs * (prob_grad - delta)).astype(jnp.bfloat16)
            dq = dq + jnp.dot(score_grad, k, preferred_element_type=f32)
            dk = scale * lax.dot_general(
                score_grad, q, (((0,), (0,)), ((), ())), preferred_element_type=f32
            )
            dv = lax.dot_general(
                probs.astype(jnp.bfloat16), do, (((0,), (0,)), ((), ())), preferred_element_type=f32
            )
            for b in range(chunk_blocks):
                block = c * chunk_blocks + b
                piece = slice(b * tok_rows, (b + 1) * tok_rows)
                if block == 0:
                    own_part_ref[g] = dk[piece]
                    own_part_ref[kv_heads + g] = dv[piece]
                else:
                    parts_ref[block - 1, g] = dk[piece].astype(jnp.bfloat16)
                    parts_ref[block - 1, kv_heads + g] = dv[piece].astype(jnp.bfloat16)
                if block == blocks // 2:
                    mirror_part_ref[g] = dk[piece]
                    mirror_part_ref[kv_heads + g] = dv[piece]
        dq_ref[heads] = (scale * dq).reshape(heads_per_group, tok_rows, head_width)


def local_backward(offsets, own_offset, q_t, do_t, fo_t, gathered, kv_heads):
    q_heads, tok_rows, head_width = q_t.shape
    blocks = gathered.shape[0]
    chunk_blocks = min(CHUNK_BLOCKS, blocks)
    rows = q_heads * tok_rows
    keys = blocks * tok_rows
    smem = pl.BlockSpec(memory_space=pltpu.SMEM)
    vmem = pl.BlockSpec(memory_space=pltpu.VMEM)
    return pl.pallas_call(
        functools.partial(backward_kernel, kv_heads=kv_heads, chunk_blocks=chunk_blocks),
        out_shape=(
            jax.ShapeDtypeStruct((q_heads, tok_rows, head_width), jnp.float32),
            jax.ShapeDtypeStruct((2 * kv_heads, tok_rows, head_width), jnp.float32),
            jax.ShapeDtypeStruct((2 * kv_heads, tok_rows, head_width), jnp.float32),
            jax.ShapeDtypeStruct((blocks - 1, 2 * kv_heads, tok_rows, head_width), jnp.bfloat16),
        ),
        in_specs=[smem, smem, vmem, vmem, vmem, vmem],
        out_specs=(vmem, vmem, vmem, vmem),
        compiler_params=pltpu.CompilerParams(vmem_limit_bytes=48 * 1024 * 1024),
        cost_estimate=pl.CostEstimate(
            flops=12 * rows * keys * head_width,
            transcendentals=2 * rows * keys,
            bytes_accessed=gathered.size * 2 + 3 * q_t.size * 2 + 6 * q_t.size,
        ),
    )(offsets, own_offset, q_t, do_t, fo_t, gathered)


def on_device(query_vectors, key_vectors, value_rows, forward_out, out_grad, block_offsets):
    tok_rows, q_heads, head_width = query_vectors.shape
    kv_heads = key_vectors.shape[1]
    cycle_size = lax.axis_size("ctx")
    kv_rows = tok_rows * kv_heads

    offset_rows = jnp.full((OFFSET_ROWS, head_width), block_offsets[0], jnp.float32).astype(jnp.bfloat16)
    paired = jnp.concatenate([key_vectors, value_rows], axis=1).transpose(1, 0, 2)
    slab = jnp.concatenate([paired.reshape(2 * kv_rows, head_width), offset_rows], axis=0)
    half = cycle_size // 2
    from_mirror = lax.ppermute(slab, "ctx", mirror_pairs(cycle_size))
    bundle = jnp.stack([slab, from_mirror])
    from_mates = [
        lax.ppermute(bundle, "ctx", mate_pairs(cycle_size, k)) for k in range(1, half)
    ]
    gathered = jnp.stack(
        [slab] + [got[0] for got in from_mates] + [from_mirror] + [got[1] for got in from_mates]
    )
    all_offsets = gathered[:, 2 * kv_rows, 0].astype(jnp.float32).astype(jnp.int32)

    dq_t, own_part, mirror_part, parts = local_backward(
        all_offsets,
        block_offsets,
        query_vectors.transpose(1, 0, 2),
        out_grad.transpose(1, 0, 2),
        forward_out.transpose(1, 0, 2),
        gathered,
        kv_heads,
    )
    own_total = own_part
    mirror_total = mirror_part
    for k in range(1, half):
        pair = jnp.stack([parts[k - 1], parts[half + k - 1]])
        arrived = lax.ppermute(pair, "ctx", mate_pairs(cycle_size, half - k)).astype(jnp.float32)
        own_total = own_total + arrived[0]
        mirror_total = mirror_total + arrived[1]
    crossed = lax.ppermute(mirror_total.astype(jnp.bfloat16), "ctx", mirror_pairs(cycle_size))
    total = own_total + crossed.astype(jnp.float32)
    key_grad = total[:kv_heads].transpose(1, 0, 2)
    value_grad = total[kv_heads:].transpose(1, 0, 2)
    return (dq_t.transpose(1, 0, 2), key_grad, value_grad)


def solution(mesh):
    in_specs = (
        P(("groups", "ctx"), "heads", None),
        P(("groups", "ctx"), "heads", None),
        P(("groups", "ctx"), "heads", None),
        P(("groups", "ctx"), "heads", None),
        P(("groups", "ctx"), "heads", None),
        P(("groups", "ctx")),
    )
    out_specs = (
        P(("groups", "ctx"), "heads", None),
        P(("groups", "ctx"), "heads", None),
        P(("groups", "ctx"), "heads", None),
    )
    return jax.shard_map(
        on_device, mesh=mesh, in_specs=in_specs, out_specs=out_specs, check_vma=False
    )
```

```python
import functools

import jax
import jax.numpy as jnp
from jax import lax
from jax.experimental import pallas as pl
from jax.experimental.pallas import tpu as pltpu
from jax.sharding import PartitionSpec as P

OFFSET_ROWS = 16
CHUNK_BLOCKS = 8
MASKED = -1e30


def mate_pairs(peers, by):
    half = peers // 2
    return [(i, half * (i // half) + (i % half + by) % half) for i in range(peers)]


def mirror_pairs(peers):
    return [(i, (i + peers // 2) % peers) for i in range(peers)]


def backward_kernel(
    offs_ref, own_ref, q_ref, do_ref, fo_ref, kv_ref, dq_ref, own_part_ref, mirror_part_ref,
    parts_ref, *, kv_heads, chunk_blocks
):
    q_heads, tok_rows, head_width = q_ref.shape
    blocks = kv_ref.shape[0]
    heads_per_group = q_heads // kv_heads
    rows = heads_per_group * tok_rows
    chunk_keys = chunk_blocks * tok_rows
    shift = tok_rows.bit_length() - 1
    scale = head_width ** (-0.5)
    f32 = jnp.float32
    row_pos = own_ref[0] * tok_rows + (
        lax.broadcasted_iota(jnp.int32, (rows, 1), 0) & (tok_rows - 1)
    )
    lane = lax.broadcasted_iota(jnp.int32, (1, chunk_keys), 1)
    lane_block = lax.shift_right_logical(lane, shift)
    lane_row = lane & (tok_rows - 1)

    def chunk_keys_of(c, g):
        k = kv_ref[c * chunk_blocks : (c + 1) * chunk_blocks, g * tok_rows : (g + 1) * tok_rows, :]
        return k.reshape(chunk_keys, head_width)

    def chunk_values_of(c, g):
        base = kv_heads * tok_rows + g * tok_rows
        v = kv_ref[c * chunk_blocks : (c + 1) * chunk_blocks, base : base + tok_rows, :]
        return v.reshape(chunk_keys, head_width)

    def chunk_scores(q, k, c):
        s = lax.dot_general(q, k, (((1,), (1,)), ((), ())), preferred_element_type=f32) * scale
        key_off = jnp.zeros((1, chunk_keys), jnp.int32)
        for b in range(chunk_blocks):
            key_off = jnp.where(lane_block == b, offs_ref[c * chunk_blocks + b], key_off)
        visible = (key_off * tok_rows + lane_row) <= row_pos
        return jnp.where(visible, s, MASKED), visible

    for g in range(kv_heads):
        heads = slice(g * heads_per_group, (g + 1) * heads_per_group)
        q = q_ref[heads].reshape(rows, head_width)
        do = do_ref[heads].reshape(rows, head_width)
        fo = fo_ref[heads].reshape(rows, head_width)
        delta = jnp.sum(do.astype(f32) * fo.astype(f32), axis=1, keepdims=True)

        run_max = jnp.full((rows, 1), MASKED, f32)
        run_total = jnp.zeros((rows, 1), f32)
        single = blocks == chunk_blocks
        for c in range(blocks // chunk_blocks):
            s, visible = chunk_scores(q, chunk_keys_of(c, g), c)
            new_max = jnp.maximum(run_max, jnp.max(s, axis=1, keepdims=True))
            run_total = run_total * jnp.exp(run_max - new_max) + jnp.sum(
                jnp.exp(s - new_max), axis=1, keepdims=True
            )
            run_max = new_max
        log_total = run_max + jnp.log(run_total)

        dq = jnp.zeros((rows, head_width), f32)
        for c in range(blocks // chunk_blocks):
            k = chunk_keys_of(c, g)
            v = chunk_values_of(c, g)
            if not single:
                s, visible = chunk_scores(q, k, c)
            probs = jnp.where(visible, jnp.exp(s - log_total), 0.0)
            prob_grad = lax.dot_general(
                do, v, (((1,), (1,)), ((), ())), preferred_element_type=f32
            )
            score_grad = (probs * (prob_grad - delta)).astype(jnp.bfloat16)
            dq = dq + jnp.dot(score_grad, k, preferred_element_type=f32)
            dk = scale * lax.dot_general(
                score_grad, q, (((0,), (0,)), ((), ())), preferred_element_type=f32
            )
            dv = lax.dot_general(
                probs.astype(jnp.bfloat16), do, (((0,), (0,)), ((), ())), preferred_element_type=f32
            )
            for b in range(chunk_blocks):
                block = c * chunk_blocks + b
                piece = slice(b * tok_rows, (b + 1) * tok_rows)
                if block == 0:
                    own_part_ref[g] = dk[piece]
                    own_part_ref[kv_heads + g] = dv[piece]
                else:
                    parts_ref[block - 1, g] = dk[piece].astype(jnp.bfloat16)
                    parts_ref[block - 1, kv_heads + g] = dv[piece].astype(jnp.bfloat16)
                if block == blocks // 2:
                    mirror_part_ref[g] = dk[piece]
                    mirror_part_ref[kv_heads + g] = dv[piece]
        dq_ref[heads] = (scale * dq).reshape(heads_per_group, tok_rows, head_width)


def local_backward(offsets, own_offset, q_t, do_t, fo_t, gathered, kv_heads):
    q_heads, tok_rows, head_width = q_t.shape
    blocks = gathered.shape[0]
    chunk_blocks = min(CHUNK_BLOCKS, blocks)
    rows = q_heads * tok_rows
    keys = blocks * tok_rows
    smem = pl.BlockSpec(memory_space=pltpu.SMEM)
    vmem = pl.BlockSpec(memory_space=pltpu.VMEM)
    return pl.pallas_call(
        functools.partial(backward_kernel, kv_heads=kv_heads, chunk_blocks=chunk_blocks),
        out_shape=(
            jax.ShapeDtypeStruct((q_heads, tok_rows, head_width), jnp.float32),
            jax.ShapeDtypeStruct((2 * kv_heads, tok_rows, head_width), jnp.float32),
            jax.ShapeDtypeStruct((2 * kv_heads, tok_rows, head_width), jnp.float32),
            jax.ShapeDtypeStruct((blocks - 1, 2 * kv_heads, tok_rows, head_width), jnp.bfloat16),
        ),
        in_specs=[smem, smem, vmem, vmem, vmem, vmem],
        out_specs=(vmem, vmem, vmem, vmem),
        compiler_params=pltpu.CompilerParams(vmem_limit_bytes=48 * 1024 * 1024),
        cost_estimate=pl.CostEstimate(
            flops=12 * rows * keys * head_width,
            transcendentals=2 * rows * keys,
            bytes_accessed=gathered.size * 2 + 3 * q_t.size * 2 + 6 * q_t.size,
        ),
    )(offsets, own_offset, q_t, do_t, fo_t, gathered)


def on_device(query_vectors, key_vectors, value_rows, forward_out, out_grad, block_offsets):
    tok_rows, q_heads, head_width = query_vectors.shape
    kv_heads = key_vectors.shape[1]
    cycle_size = lax.axis_size("ctx")
    kv_rows = tok_rows * kv_heads

    offset_rows = jnp.full((OFFSET_ROWS, head_width), block_offsets[0], jnp.float32).astype(jnp.bfloat16)
    paired = jnp.concatenate([key_vectors, value_rows], axis=1).transpose(1, 0, 2)
    slab = jnp.concatenate([paired.reshape(2 * kv_rows, head_width), offset_rows], axis=0)
    half = cycle_size // 2
    from_mates = [lax.ppermute(slab, "ctx", mate_pairs(cycle_size, k)) for k in range(1, half)]
    from_mirror = lax.ppermute(slab, "ctx", mirror_pairs(cycle_size))
    handed_on = [
        lax.ppermute(from_mirror, "ctx", mate_pairs(cycle_size, k)) for k in range(1, half)
    ]
    gathered = jnp.stack([slab] + from_mates + [from_mirror] + handed_on)
    all_offsets = gathered[:, 2 * kv_rows, 0].astype(jnp.float32).astype(jnp.int32)

    dq_t, own_part, mirror_part, parts = local_backward(
        all_offsets,
        block_offsets,
        query_vectors.transpose(1, 0, 2),
        out_grad.transpose(1, 0, 2),
        forward_out.transpose(1, 0, 2),
        gathered,
        kv_heads,
    )
    own_total = own_part
    mirror_total = mirror_part
    for k in range(1, half):
        pair = jnp.stack([parts[k - 1], parts[half + k - 1]])
        arrived = lax.ppermute(pair, "ctx", mate_pairs(cycle_size, half - k)).astype(jnp.float32)
        own_total = own_total + arrived[0]
        mirror_total = mirror_total + arrived[1]
    crossed = lax.ppermute(mirror_total.astype(jnp.bfloat16), "ctx", mirror_pairs(cycle_size))
    total = own_total + crossed.astype(jnp.float32)
    key_grad = total[:kv_heads].transpose(1, 0, 2)
    value_grad = total[kv_heads:].transpose(1, 0, 2)
    return (dq_t.transpose(1, 0, 2), key_grad, value_grad)


def solution(mesh):
    in_specs = (
        P(("groups", "ctx"), "heads", None),
        P(("groups", "ctx"), "heads", None),
        P(("groups", "ctx"), "heads", None),
        P(("groups", "ctx"), "heads", None),
        P(("groups", "ctx"), "heads", None),
        P(("groups", "ctx")),
    )
    out_specs = (
        P(("groups", "ctx"), "heads", None),
        P(("groups", "ctx"), "heads", None),
        P(("groups", "ctx"), "heads", None),
    )
    return jax.shard_map(
        on_device, mesh=mesh, in_specs=in_specs, out_specs=out_specs, check_vma=False
    )
```

```python
import functools

import jax
import jax.numpy as jnp
from jax import lax
from jax.experimental import pallas as pl
from jax.experimental.pallas import tpu as pltpu
from jax.sharding import PartitionSpec as P

OFFSET_ROWS = 16
CHUNK_BLOCKS = 8
MASKED = -1e30


def mate_pairs(peers, by):
    half = peers // 2
    return [(i, half * (i // half) + (i % half + by) % half) for i in range(peers)]


def mirror_pairs(peers):
    return [(i, (i + peers // 2) % peers) for i in range(peers)]


def backward_kernel(
    offs_ref, own_ref, q_ref, do_ref, fo_ref, kv_ref, dq_ref, own_part_ref, mirror_part_ref,
    parts_ref, *, kv_heads, chunk_blocks
):
    q_heads, tok_rows, head_width = q_ref.shape
    blocks = kv_ref.shape[0]
    heads_per_group = q_heads // kv_heads
    rows = heads_per_group * tok_rows
    chunk_keys = chunk_blocks * tok_rows
    shift = tok_rows.bit_length() - 1
    scale = head_width ** (-0.5)
    f32 = jnp.float32
    row_pos = own_ref[0] * tok_rows + (
        lax.broadcasted_iota(jnp.int32, (rows, 1), 0) & (tok_rows - 1)
    )
    lane = lax.broadcasted_iota(jnp.int32, (1, chunk_keys), 1)
    lane_block = lax.shift_right_logical(lane, shift)
    lane_row = lane & (tok_rows - 1)

    def chunk_keys_of(c, g):
        k = kv_ref[c * chunk_blocks : (c + 1) * chunk_blocks, g * tok_rows : (g + 1) * tok_rows, :]
        return k.reshape(chunk_keys, head_width)

    def chunk_values_of(c, g):
        base = kv_heads * tok_rows + g * tok_rows
        v = kv_ref[c * chunk_blocks : (c + 1) * chunk_blocks, base : base + tok_rows, :]
        return v.reshape(chunk_keys, head_width)

    def chunk_scores(q, k, c):
        s = lax.dot_general(q, k, (((1,), (1,)), ((), ())), preferred_element_type=f32) * scale
        key_off = jnp.zeros((1, chunk_keys), jnp.int32)
        for b in range(chunk_blocks):
            key_off = jnp.where(lane_block == b, offs_ref[c * chunk_blocks + b], key_off)
        visible = (key_off * tok_rows + lane_row) <= row_pos
        return jnp.where(visible, s, MASKED), visible

    for g in range(kv_heads):
        heads = slice(g * heads_per_group, (g + 1) * heads_per_group)
        q = q_ref[heads].reshape(rows, head_width)
        do = do_ref[heads].reshape(rows, head_width)
        fo = fo_ref[heads].reshape(rows, head_width)
        delta = jnp.sum(do.astype(f32) * fo.astype(f32), axis=1, keepdims=True)

        run_max = jnp.full((rows, 1), MASKED, f32)
        run_total = jnp.zeros((rows, 1), f32)
        single = blocks == chunk_blocks
        for c in range(blocks // chunk_blocks):
            s, visible = chunk_scores(q, chunk_keys_of(c, g), c)
            new_max = jnp.maximum(run_max, jnp.max(s, axis=1, keepdims=True))
            lifted = jnp.exp(s - new_max)
            run_total = run_total * jnp.exp(run_max - new_max) + jnp.sum(
                lifted, axis=1, keepdims=True
            )
            run_max = new_max
        log_total = run_max + jnp.log(run_total)

        dq = jnp.zeros((rows, head_width), f32)
        for c in range(blocks // chunk_blocks):
            k = chunk_keys_of(c, g)
            v = chunk_values_of(c, g)
            if single:
                probs = lifted * (1.0 / run_total)
            else:
                s, visible = chunk_scores(q, k, c)
                probs = jnp.exp(s - log_total)
            prob_grad = lax.dot_general(
                do, v, (((1,), (1,)), ((), ())), preferred_element_type=f32
            )
            score_grad = (probs * (prob_grad - delta)).astype(jnp.bfloat16)
            dq = dq + jnp.dot(score_grad, k, preferred_element_type=f32)
            dk = scale * lax.dot_general(
                q, score_grad, (((0,), (0,)), ((), ())), preferred_element_type=f32
            ).T
            dv = lax.dot_general(
                do, probs.astype(jnp.bfloat16), (((0,), (0,)), ((), ())), preferred_element_type=f32
            ).T
            for b in range(chunk_blocks):
                block = c * chunk_blocks + b
                piece = slice(b * tok_rows, (b + 1) * tok_rows)
                if block == 0:
                    own_part_ref[g] = dk[piece]
                    own_part_ref[kv_heads + g] = dv[piece]
                else:
                    parts_ref[block - 1, g] = dk[piece].astype(jnp.bfloat16)
                    parts_ref[block - 1, kv_heads + g] = dv[piece].astype(jnp.bfloat16)
                if block == blocks // 2:
                    mirror_part_ref[g] = dk[piece]
                    mirror_part_ref[kv_heads + g] = dv[piece]
        dq_ref[heads] = (scale * dq).reshape(heads_per_group, tok_rows, head_width)


def local_backward(offsets, own_offset, q_t, do_t, fo_t, gathered, kv_heads):
    q_heads, tok_rows, head_width = q_t.shape
    blocks = gathered.shape[0]
    chunk_blocks = min(CHUNK_BLOCKS, blocks)
    rows = q_heads * tok_rows
    keys = blocks * tok_rows
    smem = pl.BlockSpec(memory_space=pltpu.SMEM)
    vmem = pl.BlockSpec(memory_space=pltpu.VMEM)
    return pl.pallas_call(
        functools.partial(backward_kernel, kv_heads=kv_heads, chunk_blocks=chunk_blocks),
        out_shape=(
            jax.ShapeDtypeStruct((q_heads, tok_rows, head_width), jnp.float32),
            jax.ShapeDtypeStruct((2 * kv_heads, tok_rows, head_width), jnp.float32),
            jax.ShapeDtypeStruct((2 * kv_heads, tok_rows, head_width), jnp.float32),
            jax.ShapeDtypeStruct((blocks - 1, 2 * kv_heads, tok_rows, head_width), jnp.bfloat16),
        ),
        in_specs=[smem, smem, vmem, vmem, vmem, vmem],
        out_specs=(vmem, vmem, vmem, vmem),
        compiler_params=pltpu.CompilerParams(vmem_limit_bytes=48 * 1024 * 1024),
        cost_estimate=pl.CostEstimate(
            flops=12 * rows * keys * head_width,
            transcendentals=2 * rows * keys,
            bytes_accessed=gathered.size * 2 + 3 * q_t.size * 2 + 6 * q_t.size,
        ),
    )(offsets, own_offset, q_t, do_t, fo_t, gathered)


def on_device(query_vectors, key_vectors, value_rows, forward_out, out_grad, block_offsets):
    tok_rows, q_heads, head_width = query_vectors.shape
    kv_heads = key_vectors.shape[1]
    cycle_size = lax.axis_size("ctx")
    kv_rows = tok_rows * kv_heads

    offset_rows = jnp.full((OFFSET_ROWS, head_width), block_offsets[0], jnp.float32).astype(jnp.bfloat16)
    paired = jnp.concatenate([key_vectors, value_rows], axis=1).transpose(1, 0, 2)
    slab = jnp.concatenate([paired.reshape(2 * kv_rows, head_width), offset_rows], axis=0)
    half = cycle_size // 2
    from_mates = [lax.ppermute(slab, "ctx", mate_pairs(cycle_size, k)) for k in range(1, half)]
    from_mirror = lax.ppermute(slab, "ctx", mirror_pairs(cycle_size))
    handed_on = [
        lax.ppermute(from_mirror, "ctx", mate_pairs(cycle_size, k)) for k in range(1, half)
    ]
    gathered = jnp.stack([slab] + from_mates + [from_mirror] + handed_on)
    all_offsets = gathered[:, 2 * kv_rows, 0].astype(jnp.float32).astype(jnp.int32)

    dq_t, own_part, mirror_part, parts = local_backward(
        all_offsets,
        block_offsets,
        query_vectors.transpose(1, 0, 2),
        out_grad.transpose(1, 0, 2),
        forward_out.transpose(1, 0, 2),
        gathered,
        kv_heads,
    )
    own_total = own_part
    mirror_total = mirror_part
    for k in range(1, half):
        pair = jnp.stack([parts[k - 1], parts[half + k - 1]])
        arrived = lax.ppermute(pair, "ctx", mate_pairs(cycle_size, half - k)).astype(jnp.float32)
        own_total = own_total + arrived[0]
        mirror_total = mirror_total + arrived[1]
    crossed = lax.ppermute(mirror_total.astype(jnp.bfloat16), "ctx", mirror_pairs(cycle_size))
    total = own_total + crossed.astype(jnp.float32)
    key_grad = total[:kv_heads].transpose(1, 0, 2)
    value_grad = total[kv_heads:].transpose(1, 0, 2)
    return (dq_t.transpose(1, 0, 2), key_grad, value_grad)


def solution(mesh):
    in_specs = (
        P(("groups", "ctx"), "heads", None),
        P(("groups", "ctx"), "heads", None),
        P(("groups", "ctx"), "heads", None),
        P(("groups", "ctx"), "heads", None),
        P(("groups", "ctx"), "heads", None),
        P(("groups", "ctx")),
    )
    out_specs = (
        P(("groups", "ctx"), "heads", None),
        P(("groups", "ctx"), "heads", None),
        P(("groups", "ctx"), "heads", None),
    )
    return jax.shard_map(
        on_device, mesh=mesh, in_specs=in_specs, out_specs=out_specs, check_vma=False
    )
```

```python
import functools

import jax
import jax.numpy as jnp
from jax import lax
from jax.experimental import pallas as pl
from jax.experimental.pallas import tpu as pltpu
from jax.sharding import PartitionSpec as P

OFFSET_ROWS = 16
CHUNK_BLOCKS = 8
MASKED = -1e30


def mate_pairs(peers, by):
    half = peers // 2
    assert half & (half - 1) == 0
    return [(i, half * (i // half) + ((i % half) ^ by)) for i in range(peers)]


def mirror_pairs(peers):
    return [(i, (i + peers // 2) % peers) for i in range(peers)]


def backward_kernel(
    offs_ref, own_ref, q_ref, do_ref, fo_ref, kv_ref, dq_ref, own_part_ref, mirror_part_ref,
    parts_ref, *, kv_heads, chunk_blocks
):
    q_heads, tok_rows, head_width = q_ref.shape
    blocks = kv_ref.shape[0]
    heads_per_group = q_heads // kv_heads
    rows = heads_per_group * tok_rows
    chunk_keys = chunk_blocks * tok_rows
    shift = tok_rows.bit_length() - 1
    scale = head_width ** (-0.5)
    f32 = jnp.float32
    row_pos = own_ref[0] * tok_rows + (
        lax.broadcasted_iota(jnp.int32, (rows, 1), 0) & (tok_rows - 1)
    )
    lane = lax.broadcasted_iota(jnp.int32, (1, chunk_keys), 1)
    lane_block = lax.shift_right_logical(lane, shift)
    lane_row = lane & (tok_rows - 1)

    def chunk_keys_of(c, g):
        k = kv_ref[c * chunk_blocks : (c + 1) * chunk_blocks, g * tok_rows : (g + 1) * tok_rows, :]
        return k.reshape(chunk_keys, head_width)

    def chunk_values_of(c, g):
        base = kv_heads * tok_rows + g * tok_rows
        v = kv_ref[c * chunk_blocks : (c + 1) * chunk_blocks, base : base + tok_rows, :]
        return v.reshape(chunk_keys, head_width)

    def chunk_scores(q, k, c):
        s = lax.dot_general(q, k, (((1,), (1,)), ((), ())), preferred_element_type=f32) * scale
        key_off = jnp.zeros((1, chunk_keys), jnp.int32)
        for b in range(chunk_blocks):
            key_off = jnp.where(lane_block == b, offs_ref[c * chunk_blocks + b], key_off)
        visible = (key_off * tok_rows + lane_row) <= row_pos
        return jnp.where(visible, s, MASKED), visible

    for g in range(kv_heads):
        heads = slice(g * heads_per_group, (g + 1) * heads_per_group)
        q = q_ref[heads].reshape(rows, head_width)
        do = do_ref[heads].reshape(rows, head_width)
        fo = fo_ref[heads].reshape(rows, head_width)
        delta = jnp.sum(do.astype(f32) * fo.astype(f32), axis=1, keepdims=True)

        run_max = jnp.full((rows, 1), MASKED, f32)
        run_total = jnp.zeros((rows, 1), f32)
        single = blocks == chunk_blocks
        for c in range(blocks // chunk_blocks):
            s, visible = chunk_scores(q, chunk_keys_of(c, g), c)
            new_max = jnp.maximum(run_max, jnp.max(s, axis=1, keepdims=True))
            lifted = jnp.exp(s - new_max)
            run_total = run_total * jnp.exp(run_max - new_max) + jnp.sum(
                lifted, axis=1, keepdims=True
            )
            run_max = new_max
        log_total = run_max + jnp.log(run_total)

        dq = jnp.zeros((rows, head_width), f32)
        for c in range(blocks // chunk_blocks):
            k = chunk_keys_of(c, g)
            v = chunk_values_of(c, g)
            if single:
                probs = lifted * (1.0 / run_total)
            else:
                s, visible = chunk_scores(q, k, c)
                probs = jnp.exp(s - log_total)
            prob_grad = lax.dot_general(
                do, v, (((1,), (1,)), ((), ())), preferred_element_type=f32
            )
            score_grad = (probs * (prob_grad - delta)).astype(jnp.bfloat16)
            dq = dq + jnp.dot(score_grad, k, preferred_element_type=f32)
            dk = scale * lax.dot_general(
                q, score_grad, (((0,), (0,)), ((), ())), preferred_element_type=f32
            ).T
            dv = lax.dot_general(
                do, probs.astype(jnp.bfloat16), (((0,), (0,)), ((), ())), preferred_element_type=f32
            ).T
            for b in range(chunk_blocks):
                block = c * chunk_blocks + b
                piece = slice(b * tok_rows, (b + 1) * tok_rows)
                if block == 0:
                    own_part_ref[g] = dk[piece]
                    own_part_ref[kv_heads + g] = dv[piece]
                else:
                    parts_ref[block - 1, g] = dk[piece].astype(jnp.bfloat16)
                    parts_ref[block - 1, kv_heads + g] = dv[piece].astype(jnp.bfloat16)
                if block == blocks // 2:
                    mirror_part_ref[g] = dk[piece]
                    mirror_part_ref[kv_heads + g] = dv[piece]
        dq_ref[heads] = (scale * dq).reshape(heads_per_group, tok_rows, head_width)


def local_backward(offsets, own_offset, q_t, do_t, fo_t, gathered, kv_heads):
    q_heads, tok_rows, head_width = q_t.shape
    blocks = gathered.shape[0]
    chunk_blocks = min(CHUNK_BLOCKS, blocks)
    rows = q_heads * tok_rows
    keys = blocks * tok_rows
    smem = pl.BlockSpec(memory_space=pltpu.SMEM)
    vmem = pl.BlockSpec(memory_space=pltpu.VMEM)
    return pl.pallas_call(
        functools.partial(backward_kernel, kv_heads=kv_heads, chunk_blocks=chunk_blocks),
        out_shape=(
            jax.ShapeDtypeStruct((q_heads, tok_rows, head_width), jnp.float32),
            jax.ShapeDtypeStruct((2 * kv_heads, tok_rows, head_width), jnp.float32),
            jax.ShapeDtypeStruct((2 * kv_heads, tok_rows, head_width), jnp.float32),
            jax.ShapeDtypeStruct((blocks - 1, 2 * kv_heads, tok_rows, head_width), jnp.bfloat16),
        ),
        in_specs=[smem, smem, vmem, vmem, vmem, vmem],
        out_specs=(vmem, vmem, vmem, vmem),
        compiler_params=pltpu.CompilerParams(vmem_limit_bytes=48 * 1024 * 1024),
        cost_estimate=pl.CostEstimate(
            flops=12 * rows * keys * head_width,
            transcendentals=2 * rows * keys,
            bytes_accessed=gathered.size * 2 + 3 * q_t.size * 2 + 6 * q_t.size,
        ),
    )(offsets, own_offset, q_t, do_t, fo_t, gathered)


def on_device(query_vectors, key_vectors, value_rows, forward_out, out_grad, block_offsets):
    tok_rows, q_heads, head_width = query_vectors.shape
    kv_heads = key_vectors.shape[1]
    cycle_size = lax.axis_size("ctx")
    kv_rows = tok_rows * kv_heads

    offset_rows = jnp.full((OFFSET_ROWS, head_width), block_offsets[0], jnp.float32).astype(jnp.bfloat16)
    paired = jnp.concatenate([key_vectors, value_rows], axis=1).transpose(1, 0, 2)
    slab = jnp.concatenate([paired.reshape(2 * kv_rows, head_width), offset_rows], axis=0)
    half = cycle_size // 2
    from_mirror = lax.ppermute(slab, "ctx", mirror_pairs(cycle_size))
    if half == 4:
        from_x1 = lax.ppermute(slab, "ctx", mate_pairs(cycle_size, 1))
        from_x2 = lax.ppermute(slab, "ctx", mate_pairs(cycle_size, 2))
        pair = lax.ppermute(jnp.stack([from_mirror, from_x2]), "ctx", mate_pairs(cycle_size, 1))
        mirror_of_x2 = lax.ppermute(from_mirror, "ctx", mate_pairs(cycle_size, 2))
        mirror_of_x3 = lax.ppermute(from_mirror, "ctx", mate_pairs(cycle_size, 3))
        blocks = [slab, from_x1, from_x2, pair[1], from_mirror, pair[0], mirror_of_x2, mirror_of_x3]
    else:
        from_mates = [lax.ppermute(slab, "ctx", mate_pairs(cycle_size, k)) for k in range(1, half)]
        handed_on = [
            lax.ppermute(from_mirror, "ctx", mate_pairs(cycle_size, k)) for k in range(1, half)
        ]
        blocks = [slab] + from_mates + [from_mirror] + handed_on
    gathered = jnp.stack(blocks)
    all_offsets = gathered[:, 2 * kv_rows, 0].astype(jnp.float32).astype(jnp.int32)

    dq_t, own_part, mirror_part, parts = local_backward(
        all_offsets,
        block_offsets,
        query_vectors.transpose(1, 0, 2),
        out_grad.transpose(1, 0, 2),
        forward_out.transpose(1, 0, 2),
        gathered,
        kv_heads,
    )
    own_total = own_part
    mirror_total = mirror_part
    for k in range(1, half):
        pair = jnp.stack([parts[k - 1], parts[half + k - 1]])
        arrived = lax.ppermute(pair, "ctx", mate_pairs(cycle_size, k)).astype(jnp.float32)
        own_total = own_total + arrived[0]
        mirror_total = mirror_total + arrived[1]
    crossed = lax.ppermute(mirror_total.astype(jnp.bfloat16), "ctx", mirror_pairs(cycle_size))
    total = own_total + crossed.astype(jnp.float32)
    key_grad = total[:kv_heads].transpose(1, 0, 2)
    value_grad = total[kv_heads:].transpose(1, 0, 2)
    return (dq_t.transpose(1, 0, 2), key_grad, value_grad)


def solution(mesh):
    in_specs = (
        P(("groups", "ctx"), "heads", None),
        P(("groups", "ctx"), "heads", None),
        P(("groups", "ctx"), "heads", None),
        P(("groups", "ctx"), "heads", None),
        P(("groups", "ctx"), "heads", None),
        P(("groups", "ctx")),
    )
    out_specs = (
        P(("groups", "ctx"), "heads", None),
        P(("groups", "ctx"), "heads", None),
        P(("groups", "ctx"), "heads", None),
    )
    return jax.shard_map(
        on_device, mesh=mesh, in_specs=in_specs, out_specs=out_specs, check_vma=False
    )
```

```python
import functools

import jax
import jax.numpy as jnp
from jax import lax
from jax.experimental import pallas as pl
from jax.experimental.pallas import tpu as pltpu
from jax.sharding import PartitionSpec as P

OFFSET_ROWS = 16
CHUNK_BLOCKS = 8
MASKED = -1e30


def mate_pairs(peers, by):
    half = peers // 2
    return [(i, half * (i // half) + (i % half + by) % half) for i in range(peers)]


def mirror_pairs(peers):
    return [(i, (i + peers // 2) % peers) for i in range(peers)]


def backward_kernel(
    offs_ref, own_ref, q_ref, do_ref, fo_ref, kv_ref, dq_ref, own_part_ref, mirror_part_ref,
    parts_ref, *, kv_heads, chunk_blocks
):
    q_heads, tok_rows, head_width = q_ref.shape
    blocks = kv_ref.shape[0]
    heads_per_group = q_heads // kv_heads
    rows = heads_per_group * tok_rows
    chunk_keys = chunk_blocks * tok_rows
    shift = tok_rows.bit_length() - 1
    scale = head_width ** (-0.5)
    f32 = jnp.float32
    row_pos = own_ref[0] * tok_rows + (
        lax.broadcasted_iota(jnp.int32, (rows, 1), 0) & (tok_rows - 1)
    )
    lane = lax.broadcasted_iota(jnp.int32, (1, chunk_keys), 1)
    lane_block = lax.shift_right_logical(lane, shift)
    lane_row = lane & (tok_rows - 1)

    def chunk_keys_of(c, g):
        k = kv_ref[c * chunk_blocks : (c + 1) * chunk_blocks, g * tok_rows : (g + 1) * tok_rows, :]
        return k.reshape(chunk_keys, head_width)

    def chunk_values_of(c, g):
        base = kv_heads * tok_rows + g * tok_rows
        v = kv_ref[c * chunk_blocks : (c + 1) * chunk_blocks, base : base + tok_rows, :]
        return v.reshape(chunk_keys, head_width)

    def chunk_scores(q, k, c):
        s = lax.dot_general(q, k, (((1,), (1,)), ((), ())), preferred_element_type=f32) * scale
        key_off = jnp.zeros((1, chunk_keys), jnp.int32)
        for b in range(chunk_blocks):
            key_off = jnp.where(lane_block == b, offs_ref[c * chunk_blocks + b], key_off)
        visible = (key_off * tok_rows + lane_row) <= row_pos
        return jnp.where(visible, s, MASKED), visible

    for g in range(kv_heads):
        heads = slice(g * heads_per_group, (g + 1) * heads_per_group)
        q = q_ref[heads].reshape(rows, head_width)
        do = do_ref[heads].reshape(rows, head_width)
        fo = fo_ref[heads].reshape(rows, head_width)
        delta = jnp.sum(do.astype(f32) * fo.astype(f32), axis=1, keepdims=True)

        run_max = jnp.full((rows, 1), MASKED, f32)
        run_total = jnp.zeros((rows, 1), f32)
        single = blocks == chunk_blocks
        for c in range(blocks // chunk_blocks):
            s, visible = chunk_scores(q, chunk_keys_of(c, g), c)
            new_max = jnp.maximum(run_max, jnp.max(s, axis=1, keepdims=True))
            lifted = jnp.exp(s - new_max)
            run_total = run_total * jnp.exp(run_max - new_max) + jnp.sum(
                lifted, axis=1, keepdims=True
            )
            run_max = new_max
        log_total = run_max + jnp.log(run_total)

        dq = jnp.zeros((rows, head_width), f32)
        for c in range(blocks // chunk_blocks):
            k = chunk_keys_of(c, g)
            v = chunk_values_of(c, g)
            if single:
                probs = lifted * (1.0 / run_total)
            else:
                s, visible = chunk_scores(q, k, c)
                probs = jnp.exp(s - log_total)
            prob_grad = lax.dot_general(
                do, v, (((1,), (1,)), ((), ())), preferred_element_type=f32
            )
            score_grad = (probs * (prob_grad - delta)).astype(jnp.bfloat16)
            dq = dq + jnp.dot(score_grad, k, preferred_element_type=f32)
            dk = scale * lax.dot_general(
                q, score_grad, (((0,), (0,)), ((), ())), preferred_element_type=f32
            ).T
            dv = lax.dot_general(
                do, probs.astype(jnp.bfloat16), (((0,), (0,)), ((), ())), preferred_element_type=f32
            ).T
            for b in range(chunk_blocks):
                block = c * chunk_blocks + b
                piece = slice(b * tok_rows, (b + 1) * tok_rows)
                if block == 0:
                    own_part_ref[g] = dk[piece]
                    own_part_ref[kv_heads + g] = dv[piece]
                else:
                    parts_ref[block - 1, g] = dk[piece].astype(jnp.bfloat16)
                    parts_ref[block - 1, kv_heads + g] = dv[piece].astype(jnp.bfloat16)
                if block == blocks // 2:
                    mirror_part_ref[g] = dk[piece]
                    mirror_part_ref[kv_heads + g] = dv[piece]
        dq_ref[heads] = (scale * dq).reshape(heads_per_group, tok_rows, head_width)


def local_backward(offsets, own_offset, q_t, do_t, fo_t, gathered, kv_heads):
    q_heads, tok_rows, head_width = q_t.shape
    blocks = gathered.shape[0]
    chunk_blocks = min(CHUNK_BLOCKS, blocks)
    rows = q_heads * tok_rows
    keys = blocks * tok_rows
    smem = pl.BlockSpec(memory_space=pltpu.SMEM)
    vmem = pl.BlockSpec(memory_space=pltpu.VMEM)
    return pl.pallas_call(
        functools.partial(backward_kernel, kv_heads=kv_heads, chunk_blocks=chunk_blocks),
        out_shape=(
            jax.ShapeDtypeStruct((q_heads, tok_rows, head_width), jnp.float32),
            jax.ShapeDtypeStruct((2 * kv_heads, tok_rows, head_width), jnp.float32),
            jax.ShapeDtypeStruct((2 * kv_heads, tok_rows, head_width), jnp.float32),
            jax.ShapeDtypeStruct((blocks - 1, 2 * kv_heads, tok_rows, head_width), jnp.bfloat16),
        ),
        in_specs=[smem, smem, vmem, vmem, vmem, vmem],
        out_specs=(vmem, vmem, vmem, vmem),
        compiler_params=pltpu.CompilerParams(vmem_limit_bytes=48 * 1024 * 1024),
        cost_estimate=pl.CostEstimate(
            flops=12 * rows * keys * head_width,
            transcendentals=2 * rows * keys,
            bytes_accessed=gathered.size * 2 + 3 * q_t.size * 2 + 6 * q_t.size,
        ),
    )(offsets, own_offset, q_t, do_t, fo_t, gathered)


def finish_kernel(own_ref, crossed_ref, key_ref, value_ref):
    kv_heads = key_ref.shape[1]
    for j in range(2 * kv_heads):
        total = own_ref[j] + crossed_ref[j].astype(jnp.float32)
        out = key_ref if j < kv_heads else value_ref
        out[:, j % kv_heads, :] = total


def finish_sums(own_total, crossed, kv_heads):
    rows, tok_rows, head_width = own_total.shape
    vmem = pl.BlockSpec(memory_space=pltpu.VMEM)
    shape = jax.ShapeDtypeStruct((tok_rows, kv_heads, head_width), jnp.float32)
    return pl.pallas_call(
        finish_kernel,
        out_shape=(shape, shape),
        in_specs=[vmem, vmem],
        out_specs=(vmem, vmem),
        cost_estimate=pl.CostEstimate(
            flops=own_total.size, transcendentals=0, bytes_accessed=own_total.size * 10
        ),
    )(own_total, crossed)


def on_device(query_vectors, key_vectors, value_rows, forward_out, out_grad, block_offsets):
    tok_rows, q_heads, head_width = query_vectors.shape
    kv_heads = key_vectors.shape[1]
    cycle_size = lax.axis_size("ctx")
    kv_rows = tok_rows * kv_heads

    offset_rows = jnp.full((OFFSET_ROWS, head_width), block_offsets[0], jnp.float32).astype(jnp.bfloat16)
    paired = jnp.concatenate([key_vectors, value_rows], axis=1).transpose(1, 0, 2)
    slab = jnp.concatenate([paired.reshape(2 * kv_rows, head_width), offset_rows], axis=0)
    half = cycle_size // 2
    from_mates = [lax.ppermute(slab, "ctx", mate_pairs(cycle_size, k)) for k in range(1, half)]
    from_mirror = lax.ppermute(slab, "ctx", mirror_pairs(cycle_size))
    handed_on = [
        lax.ppermute(from_mirror, "ctx", mate_pairs(cycle_size, k)) for k in range(1, half)
    ]
    gathered = jnp.stack([slab] + from_mates + [from_mirror] + handed_on)
    all_offsets = gathered[:, 2 * kv_rows, 0].astype(jnp.float32).astype(jnp.int32)

    dq_t, own_part, mirror_part, parts = local_backward(
        all_offsets,
        block_offsets,
        query_vectors.transpose(1, 0, 2),
        out_grad.transpose(1, 0, 2),
        forward_out.transpose(1, 0, 2),
        gathered,
        kv_heads,
    )
    own_total = own_part
    mirror_total = mirror_part
    for k in range(1, half):
        pair = jnp.stack([parts[k - 1], parts[half + k - 1]])
        arrived = lax.ppermute(pair, "ctx", mate_pairs(cycle_size, half - k)).astype(jnp.float32)
        own_total = own_total + arrived[0]
        mirror_total = mirror_total + arrived[1]
    crossed = lax.ppermute(mirror_total.astype(jnp.bfloat16), "ctx", mirror_pairs(cycle_size))
    key_grad, value_grad = finish_sums(own_total, crossed, kv_heads)
    return (dq_t.transpose(1, 0, 2), key_grad, value_grad)


def solution(mesh):
    in_specs = (
        P(("groups", "ctx"), "heads", None),
        P(("groups", "ctx"), "heads", None),
        P(("groups", "ctx"), "heads", None),
        P(("groups", "ctx"), "heads", None),
        P(("groups", "ctx"), "heads", None),
        P(("groups", "ctx")),
    )
    out_specs = (
        P(("groups", "ctx"), "heads", None),
        P(("groups", "ctx"), "heads", None),
        P(("groups", "ctx"), "heads", None),
    )
    return jax.shard_map(
        on_device, mesh=mesh, in_specs=in_specs, out_specs=out_specs, check_vma=False
    )
```

```python
import functools

import jax
import jax.numpy as jnp
from jax import lax
from jax.experimental import pallas as pl
from jax.experimental.pallas import tpu as pltpu
from jax.sharding import PartitionSpec as P

OFFSET_ROWS = 16
CHUNK_BLOCKS = 8
MASKED = -1e30


def mate_pairs(peers, by):
    half = peers // 2
    assert half & (half - 1) == 0
    return [(i, half * (i // half) + ((i % half) ^ by)) for i in range(peers)]


def mirror_pairs(peers):
    return [(i, (i + peers // 2) % peers) for i in range(peers)]


def backward_kernel(
    offs_ref, own_ref, q_ref, do_ref, fo_ref, kv_ref, dq_ref, own_part_ref, mirror_part_ref,
    parts_ref, *, kv_heads, chunk_blocks
):
    q_heads, tok_rows, head_width = q_ref.shape
    blocks = kv_ref.shape[0]
    heads_per_group = q_heads // kv_heads
    rows = heads_per_group * tok_rows
    chunk_keys = chunk_blocks * tok_rows
    shift = tok_rows.bit_length() - 1
    scale = head_width ** (-0.5)
    f32 = jnp.float32
    row_pos = own_ref[0] * tok_rows + (
        lax.broadcasted_iota(jnp.int32, (rows, 1), 0) & (tok_rows - 1)
    )
    lane = lax.broadcasted_iota(jnp.int32, (1, chunk_keys), 1)
    lane_block = lax.shift_right_logical(lane, shift)
    lane_row = lane & (tok_rows - 1)

    def chunk_keys_of(c, g):
        k = kv_ref[c * chunk_blocks : (c + 1) * chunk_blocks, g * tok_rows : (g + 1) * tok_rows, :]
        return k.reshape(chunk_keys, head_width)

    def chunk_values_of(c, g):
        base = kv_heads * tok_rows + g * tok_rows
        v = kv_ref[c * chunk_blocks : (c + 1) * chunk_blocks, base : base + tok_rows, :]
        return v.reshape(chunk_keys, head_width)

    def chunk_scores(q, k, c):
        s = lax.dot_general(q, k, (((1,), (1,)), ((), ())), preferred_element_type=f32) * scale
        key_off = jnp.zeros((1, chunk_keys), jnp.int32)
        for b in range(chunk_blocks):
            key_off = jnp.where(lane_block == b, offs_ref[c * chunk_blocks + b], key_off)
        visible = (key_off * tok_rows + lane_row) <= row_pos
        return jnp.where(visible, s, MASKED), visible

    for g in range(kv_heads):
        heads = slice(g * heads_per_group, (g + 1) * heads_per_group)
        q = q_ref[heads].reshape(rows, head_width)
        do = do_ref[heads].reshape(rows, head_width)
        fo = fo_ref[heads].reshape(rows, head_width)
        delta = jnp.sum(do.astype(f32) * fo.astype(f32), axis=1, keepdims=True)

        run_max = jnp.full((rows, 1), MASKED, f32)
        run_total = jnp.zeros((rows, 1), f32)
        single = blocks == chunk_blocks
        for c in range(blocks // chunk_blocks):
            s, visible = chunk_scores(q, chunk_keys_of(c, g), c)
            new_max = jnp.maximum(run_max, jnp.max(s, axis=1, keepdims=True))
            lifted = jnp.exp(s - new_max)
            run_total = run_total * jnp.exp(run_max - new_max) + jnp.sum(
                lifted, axis=1, keepdims=True
            )
            run_max = new_max
        log_total = run_max + jnp.log(run_total)

        dq = jnp.zeros((rows, head_width), f32)
        for c in range(blocks // chunk_blocks):
            k = chunk_keys_of(c, g)
            v = chunk_values_of(c, g)
            if single:
                probs = lifted * (1.0 / run_total)
            else:
                s, visible = chunk_scores(q, k, c)
                probs = jnp.exp(s - log_total)
            prob_grad = lax.dot_general(
                do, v, (((1,), (1,)), ((), ())), preferred_element_type=f32
            )
            score_grad = (probs * (prob_grad - delta)).astype(jnp.bfloat16)
            dq = dq + jnp.dot(score_grad, k, preferred_element_type=f32)
            dk = scale * lax.dot_general(
                q, score_grad, (((0,), (0,)), ((), ())), preferred_element_type=f32
            ).T
            dv = lax.dot_general(
                do, probs.astype(jnp.bfloat16), (((0,), (0,)), ((), ())), preferred_element_type=f32
            ).T
            for b in range(chunk_blocks):
                block = c * chunk_blocks + b
                piece = slice(b * tok_rows, (b + 1) * tok_rows)
                if block == 0:
                    own_part_ref[g] = dk[piece]
                    own_part_ref[kv_heads + g] = dv[piece]
                else:
                    parts_ref[block - 1, g] = dk[piece].astype(jnp.bfloat16)
                    parts_ref[block - 1, kv_heads + g] = dv[piece].astype(jnp.bfloat16)
                if block == blocks // 2:
                    mirror_part_ref[g] = dk[piece]
                    mirror_part_ref[kv_heads + g] = dv[piece]
        dq_ref[heads] = (scale * dq).reshape(heads_per_group, tok_rows, head_width)


def local_backward(offsets, own_offset, q_t, do_t, fo_t, gathered, kv_heads):
    q_heads, tok_rows, head_width = q_t.shape
    blocks = gathered.shape[0]
    chunk_blocks = min(CHUNK_BLOCKS, blocks)
    rows = q_heads * tok_rows
    keys = blocks * tok_rows
    smem = pl.BlockSpec(memory_space=pltpu.SMEM)
    vmem = pl.BlockSpec(memory_space=pltpu.VMEM)
    return pl.pallas_call(
        functools.partial(backward_kernel, kv_heads=kv_heads, chunk_blocks=chunk_blocks),
        out_shape=(
            jax.ShapeDtypeStruct((q_heads, tok_rows, head_width), jnp.float32),
            jax.ShapeDtypeStruct((2 * kv_heads, tok_rows, head_width), jnp.float32),
            jax.ShapeDtypeStruct((2 * kv_heads, tok_rows, head_width), jnp.float32),
            jax.ShapeDtypeStruct((blocks - 1, 2 * kv_heads, tok_rows, head_width), jnp.bfloat16),
        ),
        in_specs=[smem, smem, vmem, vmem, vmem, vmem],
        out_specs=(vmem, vmem, vmem, vmem),
        compiler_params=pltpu.CompilerParams(vmem_limit_bytes=48 * 1024 * 1024),
        cost_estimate=pl.CostEstimate(
            flops=12 * rows * keys * head_width,
            transcendentals=2 * rows * keys,
            bytes_accessed=gathered.size * 2 + 3 * q_t.size * 2 + 6 * q_t.size,
        ),
    )(offsets, own_offset, q_t, do_t, fo_t, gathered)


def on_device(query_vectors, key_vectors, value_rows, forward_out, out_grad, block_offsets):
    tok_rows, q_heads, head_width = query_vectors.shape
    kv_heads = key_vectors.shape[1]
    cycle_size = lax.axis_size("ctx")
    kv_rows = tok_rows * kv_heads

    offset_rows = jnp.full((OFFSET_ROWS, head_width), block_offsets[0], jnp.float32).astype(jnp.bfloat16)
    paired = jnp.concatenate([key_vectors, value_rows], axis=1).transpose(1, 0, 2)
    slab = jnp.concatenate([paired.reshape(2 * kv_rows, head_width), offset_rows], axis=0)
    half = cycle_size // 2
    from_mirror = lax.ppermute(slab, "ctx", mirror_pairs(cycle_size))
    if half == 4:
        across_pairs = [(i, half * (j // half) + ((j % half) ^ 1)) for i, j in mirror_pairs(cycle_size)]
        from_mirror_x1 = lax.ppermute(slab, "ctx", across_pairs)
        from_x1 = lax.ppermute(slab, "ctx", mate_pairs(cycle_size, 1))
        from_x2 = lax.ppermute(slab, "ctx", mate_pairs(cycle_size, 2))
        from_x3 = lax.ppermute(slab, "ctx", mate_pairs(cycle_size, 3))
        pair = lax.ppermute(
            jnp.stack([from_mirror, from_mirror_x1]), "ctx", mate_pairs(cycle_size, 2)
        )
        blocks = [slab, from_x1, from_x2, from_x3, from_mirror, from_mirror_x1, pair[0], pair[1]]
    else:
        from_mates = [lax.ppermute(slab, "ctx", mate_pairs(cycle_size, k)) for k in range(1, half)]
        handed_on = [
            lax.ppermute(from_mirror, "ctx", mate_pairs(cycle_size, k)) for k in range(1, half)
        ]
        blocks = [slab] + from_mates + [from_mirror] + handed_on
    gathered = jnp.stack(blocks)
    all_offsets = gathered[:, 2 * kv_rows, 0].astype(jnp.float32).astype(jnp.int32)

    dq_t, own_part, mirror_part, parts = local_backward(
        all_offsets,
        block_offsets,
        query_vectors.transpose(1, 0, 2),
        out_grad.transpose(1, 0, 2),
        forward_out.transpose(1, 0, 2),
        gathered,
        kv_heads,
    )
    own_total = own_part
    mirror_total = mirror_part
    for k in range(1, half):
        pair = jnp.stack([parts[k - 1], parts[half + k - 1]])
        arrived = lax.ppermute(pair, "ctx", mate_pairs(cycle_size, k)).astype(jnp.float32)
        own_total = own_total + arrived[0]
        mirror_total = mirror_total + arrived[1]
    crossed = lax.ppermute(mirror_total.astype(jnp.bfloat16), "ctx", mirror_pairs(cycle_size))
    total = own_total + crossed.astype(jnp.float32)
    key_grad = total[:kv_heads].transpose(1, 0, 2)
    value_grad = total[kv_heads:].transpose(1, 0, 2)
    return (dq_t.transpose(1, 0, 2), key_grad, value_grad)


def solution(mesh):
    in_specs = (
        P(("groups", "ctx"), "heads", None),
        P(("groups", "ctx"), "heads", None),
        P(("groups", "ctx"), "heads", None),
        P(("groups", "ctx"), "heads", None),
        P(("groups", "ctx"), "heads", None),
        P(("groups", "ctx")),
    )
    out_specs = (
        P(("groups", "ctx"), "heads", None),
        P(("groups", "ctx"), "heads", None),
        P(("groups", "ctx"), "heads", None),
    )
    return jax.shard_map(
        on_device, mesh=mesh, in_specs=in_specs, out_specs=out_specs, check_vma=False
    )
```

```python
import functools

import jax
import jax.numpy as jnp
from jax import lax
from jax.experimental import pallas as pl
from jax.experimental.pallas import tpu as pltpu
from jax.sharding import PartitionSpec as P

OFFSET_ROWS = 16
CHUNK_BLOCKS = 8
MASKED = -1e30


def mate_pairs(peers, by):
    half = peers // 2
    return [(i, half * (i // half) + (i % half + by) % half) for i in range(peers)]


def mirror_pairs(peers):
    return [(i, (i + peers // 2) % peers) for i in range(peers)]


def backward_kernel(
    offs_ref, own_ref, q_ref, do_ref, fo_ref, kv_ref, dq_ref, own_part_ref, mirror_part_ref,
    parts_ref, *, kv_heads, chunk_blocks
):
    q_heads, tok_rows, head_width = q_ref.shape
    blocks = kv_ref.shape[0]
    heads_per_group = q_heads // kv_heads
    rows = heads_per_group * tok_rows
    chunk_keys = chunk_blocks * tok_rows
    shift = tok_rows.bit_length() - 1
    scale = head_width ** (-0.5)
    f32 = jnp.float32
    row_pos = own_ref[0] * tok_rows + (
        lax.broadcasted_iota(jnp.int32, (rows, 1), 0) & (tok_rows - 1)
    )
    lane = lax.broadcasted_iota(jnp.int32, (1, chunk_keys), 1)
    lane_block = lax.shift_right_logical(lane, shift)
    lane_row = lane & (tok_rows - 1)

    def chunk_keys_of(c, g):
        k = kv_ref[c * chunk_blocks : (c + 1) * chunk_blocks, g * tok_rows : (g + 1) * tok_rows, :]
        return k.reshape(chunk_keys, head_width)

    def chunk_values_of(c, g):
        base = kv_heads * tok_rows + g * tok_rows
        v = kv_ref[c * chunk_blocks : (c + 1) * chunk_blocks, base : base + tok_rows, :]
        return v.reshape(chunk_keys, head_width)

    def chunk_scores(q, k, c):
        s = lax.dot_general(q, k, (((1,), (1,)), ((), ())), preferred_element_type=f32) * scale
        key_off = jnp.zeros((1, chunk_keys), jnp.int32)
        for b in range(chunk_blocks):
            key_off = jnp.where(lane_block == b, offs_ref[c * chunk_blocks + b], key_off)
        visible = (key_off * tok_rows + lane_row) <= row_pos
        return jnp.where(visible, s, MASKED), visible

    for g in range(kv_heads):
        heads = slice(g * heads_per_group, (g + 1) * heads_per_group)
        q = q_ref[heads].reshape(rows, head_width)
        do = do_ref[heads].reshape(rows, head_width)
        fo = fo_ref[heads].reshape(rows, head_width)
        delta = jnp.sum(do.astype(f32) * fo.astype(f32), axis=1, keepdims=True)

        run_max = jnp.full((rows, 1), MASKED, f32)
        run_total = jnp.zeros((rows, 1), f32)
        single = blocks == chunk_blocks
        for c in range(blocks // chunk_blocks):
            s, visible = chunk_scores(q, chunk_keys_of(c, g), c)
            new_max = jnp.maximum(run_max, jnp.max(s, axis=1, keepdims=True))
            lifted = jnp.exp(s - new_max)
            run_total = run_total * jnp.exp(run_max - new_max) + jnp.sum(
                lifted, axis=1, keepdims=True
            )
            run_max = new_max
        log_total = run_max + jnp.log(run_total)

        dq = jnp.zeros((rows, head_width), f32)
        for c in range(blocks // chunk_blocks):
            k = chunk_keys_of(c, g)
            v = chunk_values_of(c, g)
            if single:
                probs = lifted * (1.0 / run_total)
            else:
                s, visible = chunk_scores(q, k, c)
                probs = jnp.exp(s - log_total)
            prob_grad = lax.dot_general(
                do, v, (((1,), (1,)), ((), ())), preferred_element_type=f32
            )
            score_grad = (probs * (prob_grad - delta)).astype(jnp.bfloat16)
            dq = dq + jnp.dot(score_grad, k, preferred_element_type=f32)
            dk = scale * lax.dot_general(
                q, score_grad, (((0,), (0,)), ((), ())), preferred_element_type=f32
            ).T
            dv = lax.dot_general(
                do, probs.astype(jnp.bfloat16), (((0,), (0,)), ((), ())), preferred_element_type=f32
            ).T
            for b in range(chunk_blocks):
                block = c * chunk_blocks + b
                piece = slice(b * tok_rows, (b + 1) * tok_rows)
                if block == 0:
                    own_part_ref[g] = dk[piece]
                    own_part_ref[kv_heads + g] = dv[piece]
                else:
                    parts_ref[block - 1, g] = dk[piece].astype(jnp.bfloat16)
                    parts_ref[block - 1, kv_heads + g] = dv[piece].astype(jnp.bfloat16)
                if block == blocks // 2:
                    mirror_part_ref[g] = dk[piece]
                    mirror_part_ref[kv_heads + g] = dv[piece]
        dq_ref[heads] = (scale * dq).reshape(heads_per_group, tok_rows, head_width)


def local_backward(offsets, own_offset, q_t, do_t, fo_t, gathered, kv_heads):
    q_heads, tok_rows, head_width = q_t.shape
    blocks = gathered.shape[0]
    chunk_blocks = min(CHUNK_BLOCKS, blocks)
    rows = q_heads * tok_rows
    keys = blocks * tok_rows
    smem = pl.BlockSpec(memory_space=pltpu.SMEM)
    vmem = pl.BlockSpec(memory_space=pltpu.VMEM)
    return pl.pallas_call(
        functools.partial(backward_kernel, kv_heads=kv_heads, chunk_blocks=chunk_blocks),
        out_shape=(
            jax.ShapeDtypeStruct((q_heads, tok_rows, head_width), jnp.float32),
            jax.ShapeDtypeStruct((2 * kv_heads, tok_rows, head_width), jnp.float32),
            jax.ShapeDtypeStruct((2 * kv_heads, tok_rows, head_width), jnp.float32),
            jax.ShapeDtypeStruct((blocks - 1, 2 * kv_heads, tok_rows, head_width), jnp.bfloat16),
        ),
        in_specs=[smem, smem, vmem, vmem, vmem, vmem],
        out_specs=(vmem, vmem, vmem, vmem),
        compiler_params=pltpu.CompilerParams(vmem_limit_bytes=48 * 1024 * 1024),
        cost_estimate=pl.CostEstimate(
            flops=12 * rows * keys * head_width,
            transcendentals=2 * rows * keys,
            bytes_accessed=gathered.size * 2 + 3 * q_t.size * 2 + 6 * q_t.size,
        ),
    )(offsets, own_offset, q_t, do_t, fo_t, gathered)


def on_device(query_vectors, key_vectors, value_rows, forward_out, out_grad, block_offsets):
    tok_rows, q_heads, head_width = query_vectors.shape
    kv_heads = key_vectors.shape[1]
    cycle_size = lax.axis_size("ctx")
    kv_rows = tok_rows * kv_heads

    offset_rows = jnp.full((OFFSET_ROWS, head_width), block_offsets[0], jnp.float32).astype(jnp.bfloat16)
    paired = jnp.concatenate([key_vectors, value_rows], axis=1).transpose(1, 0, 2)
    slab = jnp.concatenate([paired.reshape(2 * kv_rows, head_width), offset_rows], axis=0)
    half = cycle_size // 2
    from_mates = [lax.ppermute(slab, "ctx", mate_pairs(cycle_size, k)) for k in range(1, half)]
    from_mirror = lax.ppermute(slab, "ctx", mirror_pairs(cycle_size))
    handed_on = [
        lax.ppermute(from_mirror, "ctx", mate_pairs(cycle_size, k)) for k in range(1, half)
    ]
    gathered = jnp.stack([slab] + from_mates + [from_mirror] + handed_on)
    all_offsets = gathered[:, 2 * kv_rows, 0].astype(jnp.float32).astype(jnp.int32)

    dq_t, own_part, mirror_part, parts = local_backward(
        all_offsets,
        block_offsets,
        query_vectors.transpose(1, 0, 2),
        out_grad.transpose(1, 0, 2),
        forward_out.transpose(1, 0, 2),
        gathered,
        kv_heads,
    )
    mirror_total = mirror_part
    for k in range(1, half):
        arrived = lax.ppermute(parts[half + k - 1], "ctx", mate_pairs(cycle_size, half - k))
        mirror_total = mirror_total + arrived.astype(jnp.float32)
    own_total = own_part
    for k in range(1, half):
        arrived = lax.ppermute(parts[k - 1], "ctx", mate_pairs(cycle_size, half - k))
        own_total = own_total + arrived.astype(jnp.float32)
    crossed = lax.ppermute(mirror_total.astype(jnp.bfloat16), "ctx", mirror_pairs(cycle_size))
    total = own_total + crossed.astype(jnp.float32)
    key_grad = total[:kv_heads].transpose(1, 0, 2)
    value_grad = total[kv_heads:].transpose(1, 0, 2)
    return (dq_t.transpose(1, 0, 2), key_grad, value_grad)


def solution(mesh):
    in_specs = (
        P(("groups", "ctx"), "heads", None),
        P(("groups", "ctx"), "heads", None),
        P(("groups", "ctx"), "heads", None),
        P(("groups", "ctx"), "heads", None),
        P(("groups", "ctx"), "heads", None),
        P(("groups", "ctx")),
    )
    out_specs = (
        P(("groups", "ctx"), "heads", None),
        P(("groups", "ctx"), "heads", None),
        P(("groups", "ctx"), "heads", None),
    )
    return jax.shard_map(
        on_device, mesh=mesh, in_specs=in_specs, out_specs=out_specs, check_vma=False
    )
```

```python
import functools

import jax
import jax.numpy as jnp
from jax import lax
from jax.experimental import pallas as pl
from jax.experimental.pallas import tpu as pltpu
from jax.sharding import PartitionSpec as P

OFFSET_ROWS = 16
CHUNK_BLOCKS = 8
MASKED = -1e30


def mate_pairs(peers, by):
    half = peers // 2
    assert half & (half - 1) == 0
    return [(i, half * (i // half) + ((i % half) ^ by)) for i in range(peers)]


def mirror_pairs(peers):
    return [(i, (i + peers // 2) % peers) for i in range(peers)]


def backward_kernel(
    offs_ref, own_ref, q_ref, do_ref, fo_ref, kv_ref, dq_ref, own_part_ref, mirror_part_ref,
    parts_ref, *, kv_heads, chunk_blocks
):
    q_heads, tok_rows, head_width = q_ref.shape
    blocks = kv_ref.shape[0]
    heads_per_group = q_heads // kv_heads
    rows = heads_per_group * tok_rows
    chunk_keys = chunk_blocks * tok_rows
    shift = tok_rows.bit_length() - 1
    scale = head_width ** (-0.5)
    f32 = jnp.float32
    row_pos = own_ref[0] * tok_rows + (
        lax.broadcasted_iota(jnp.int32, (rows, 1), 0) & (tok_rows - 1)
    )
    lane = lax.broadcasted_iota(jnp.int32, (1, chunk_keys), 1)
    lane_block = lax.shift_right_logical(lane, shift)
    lane_row = lane & (tok_rows - 1)

    def chunk_keys_of(c, g):
        k = kv_ref[c * chunk_blocks : (c + 1) * chunk_blocks, g * tok_rows : (g + 1) * tok_rows, :]
        return k.reshape(chunk_keys, head_width)

    def chunk_values_of(c, g):
        base = kv_heads * tok_rows + g * tok_rows
        v = kv_ref[c * chunk_blocks : (c + 1) * chunk_blocks, base : base + tok_rows, :]
        return v.reshape(chunk_keys, head_width)

    def chunk_scores(q, k, c):
        s = lax.dot_general(q, k, (((1,), (1,)), ((), ())), preferred_element_type=f32) * scale
        key_off = jnp.zeros((1, chunk_keys), jnp.int32)
        for b in range(chunk_blocks):
            key_off = jnp.where(lane_block == b, offs_ref[c * chunk_blocks + b], key_off)
        visible = (key_off * tok_rows + lane_row) <= row_pos
        return jnp.where(visible, s, MASKED), visible

    for g in range(kv_heads):
        heads = slice(g * heads_per_group, (g + 1) * heads_per_group)
        q = q_ref[heads].reshape(rows, head_width)
        do = do_ref[heads].reshape(rows, head_width)
        fo = fo_ref[heads].reshape(rows, head_width)
        delta = jnp.sum(do.astype(f32) * fo.astype(f32), axis=1, keepdims=True)

        run_max = jnp.full((rows, 1), MASKED, f32)
        run_total = jnp.zeros((rows, 1), f32)
        single = blocks == chunk_blocks
        for c in range(blocks // chunk_blocks):
            s, visible = chunk_scores(q, chunk_keys_of(c, g), c)
            new_max = jnp.maximum(run_max, jnp.max(s, axis=1, keepdims=True))
            lifted = jnp.exp(s - new_max)
            run_total = run_total * jnp.exp(run_max - new_max) + jnp.sum(
                lifted, axis=1, keepdims=True
            )
            run_max = new_max
        log_total = run_max + jnp.log(run_total)

        dq = jnp.zeros((rows, head_width), f32)
        for c in range(blocks // chunk_blocks):
            k = chunk_keys_of(c, g)
            v = chunk_values_of(c, g)
            if single:
                probs = lifted * (1.0 / run_total)
            else:
                s, visible = chunk_scores(q, k, c)
                probs = jnp.exp(s - log_total)
            prob_grad = lax.dot_general(
                do, v, (((1,), (1,)), ((), ())), preferred_element_type=f32
            )
            score_grad = (probs * (prob_grad - delta)).astype(jnp.bfloat16)
            dq = dq + jnp.dot(score_grad, k, preferred_element_type=f32)
            dk = scale * lax.dot_general(
                q, score_grad, (((0,), (0,)), ((), ())), preferred_element_type=f32
            ).T
            dv = lax.dot_general(
                do, probs.astype(jnp.bfloat16), (((0,), (0,)), ((), ())), preferred_element_type=f32
            ).T
            for b in range(chunk_blocks):
                block = c * chunk_blocks + b
                piece = slice(b * tok_rows, (b + 1) * tok_rows)
                if block == 0:
                    own_part_ref[g] = dk[piece]
                    own_part_ref[kv_heads + g] = dv[piece]
                else:
                    parts_ref[block - 1, g] = dk[piece].astype(jnp.bfloat16)
                    parts_ref[block - 1, kv_heads + g] = dv[piece].astype(jnp.bfloat16)
                if block == blocks // 2:
                    mirror_part_ref[g] = dk[piece]
                    mirror_part_ref[kv_heads + g] = dv[piece]
        dq_ref[heads] = (scale * dq).reshape(heads_per_group, tok_rows, head_width)


def local_backward(offsets, own_offset, q_t, do_t, fo_t, gathered, kv_heads):
    q_heads, tok_rows, head_width = q_t.shape
    blocks = gathered.shape[0]
    chunk_blocks = min(CHUNK_BLOCKS, blocks)
    rows = q_heads * tok_rows
    keys = blocks * tok_rows
    smem = pl.BlockSpec(memory_space=pltpu.SMEM)
    vmem = pl.BlockSpec(memory_space=pltpu.VMEM)
    return pl.pallas_call(
        functools.partial(backward_kernel, kv_heads=kv_heads, chunk_blocks=chunk_blocks),
        out_shape=(
            jax.ShapeDtypeStruct((q_heads, tok_rows, head_width), jnp.float32),
            jax.ShapeDtypeStruct((2 * kv_heads, tok_rows, head_width), jnp.float32),
            jax.ShapeDtypeStruct((2 * kv_heads, tok_rows, head_width), jnp.float32),
            jax.ShapeDtypeStruct((blocks - 1, 2 * kv_heads, tok_rows, head_width), jnp.bfloat16),
        ),
        in_specs=[smem, smem, vmem, vmem, vmem, vmem],
        out_specs=(vmem, vmem, vmem, vmem),
        compiler_params=pltpu.CompilerParams(vmem_limit_bytes=48 * 1024 * 1024),
        cost_estimate=pl.CostEstimate(
            flops=12 * rows * keys * head_width,
            transcendentals=2 * rows * keys,
            bytes_accessed=gathered.size * 2 + 3 * q_t.size * 2 + 6 * q_t.size,
        ),
    )(offsets, own_offset, q_t, do_t, fo_t, gathered)


def on_device(query_vectors, key_vectors, value_rows, forward_out, out_grad, block_offsets):
    tok_rows, q_heads, head_width = query_vectors.shape
    kv_heads = key_vectors.shape[1]
    cycle_size = lax.axis_size("ctx")
    kv_rows = tok_rows * kv_heads

    offset_rows = jnp.full((OFFSET_ROWS, head_width), block_offsets[0], jnp.float32).astype(jnp.bfloat16)
    paired = jnp.concatenate([key_vectors, value_rows], axis=1).transpose(1, 0, 2)
    slab = jnp.concatenate([paired.reshape(2 * kv_rows, head_width), offset_rows], axis=0)
    half = cycle_size // 2
    from_mirror = lax.ppermute(slab, "ctx", mirror_pairs(cycle_size))
    if half == 4:
        from_x1 = lax.ppermute(slab, "ctx", mate_pairs(cycle_size, 1))
        from_x2 = lax.ppermute(slab, "ctx", mate_pairs(cycle_size, 2))
        pair = lax.ppermute(jnp.stack([from_mirror, from_x2]), "ctx", mate_pairs(cycle_size, 1))
        mirror_of_x2 = lax.ppermute(from_mirror, "ctx", mate_pairs(cycle_size, 2))
        mirror_of_x3 = lax.ppermute(from_mirror, "ctx", mate_pairs(cycle_size, 3))
        blocks = [slab, from_x1, from_x2, pair[1], from_mirror, pair[0], mirror_of_x2, mirror_of_x3]
    else:
        from_mates = [lax.ppermute(slab, "ctx", mate_pairs(cycle_size, k)) for k in range(1, half)]
        handed_on = [
            lax.ppermute(from_mirror, "ctx", mate_pairs(cycle_size, k)) for k in range(1, half)
        ]
        blocks = [slab] + from_mates + [from_mirror] + handed_on
    gathered = jnp.stack(blocks)
    all_offsets = gathered[:, 2 * kv_rows, 0].astype(jnp.float32).astype(jnp.int32)

    dq_t, own_part, mirror_part, parts = local_backward(
        all_offsets,
        block_offsets,
        query_vectors.transpose(1, 0, 2),
        out_grad.transpose(1, 0, 2),
        forward_out.transpose(1, 0, 2),
        gathered,
        kv_heads,
    )
    mirror_total = mirror_part
    for k in range(1, half):
        arrived = lax.ppermute(parts[half + k - 1], "ctx", mate_pairs(cycle_size, k))
        mirror_total = mirror_total + arrived.astype(jnp.float32)
    own_total = own_part
    for k in range(1, half):
        arrived = lax.ppermute(parts[k - 1], "ctx", mate_pairs(cycle_size, k))
        own_total = own_total + arrived.astype(jnp.float32)
    crossed = lax.ppermute(mirror_total.astype(jnp.bfloat16), "ctx", mirror_pairs(cycle_size))
    total = own_total + crossed.astype(jnp.float32)
    key_grad = total[:kv_heads].transpose(1, 0, 2)
    value_grad = total[kv_heads:].transpose(1, 0, 2)
    return (dq_t.transpose(1, 0, 2), key_grad, value_grad)


def solution(mesh):
    in_specs = (
        P(("groups", "ctx"), "heads", None),
        P(("groups", "ctx"), "heads", None),
        P(("groups", "ctx"), "heads", None),
        P(("groups", "ctx"), "heads", None),
        P(("groups", "ctx"), "heads", None),
        P(("groups", "ctx")),
    )
    out_specs = (
        P(("groups", "ctx"), "heads", None),
        P(("groups", "ctx"), "heads", None),
        P(("groups", "ctx"), "heads", None),
    )
    return jax.shard_map(
        on_device, mesh=mesh, in_specs=in_specs, out_specs=out_specs, check_vma=False
    )
```

```python
import functools

import jax
import jax.numpy as jnp
from jax import lax
from jax.experimental import pallas as pl
from jax.experimental.pallas import tpu as pltpu
from jax.sharding import PartitionSpec as P

OFFSET_ROWS = 16
CHUNK_BLOCKS = 8
MASKED = -1e30


def mate_pairs(peers, by):
    half = peers // 2
    assert half & (half - 1) == 0
    return [(i, half * (i // half) + ((i % half) ^ by)) for i in range(peers)]


def mirror_pairs(peers):
    return [(i, (i + peers // 2) % peers) for i in range(peers)]


def backward_kernel(
    offs_ref, own_ref, q_ref, do_ref, fo_ref, kv_ref, dq_ref, own_part_ref, mirror_part_ref,
    parts_ref, *, kv_heads, chunk_blocks
):
    q_heads, tok_rows, head_width = q_ref.shape
    blocks = kv_ref.shape[0]
    heads_per_group = q_heads // kv_heads
    rows = heads_per_group * tok_rows
    chunk_keys = chunk_blocks * tok_rows
    shift = tok_rows.bit_length() - 1
    scale = head_width ** (-0.5)
    f32 = jnp.float32
    row_pos = own_ref[0] * tok_rows + (
        lax.broadcasted_iota(jnp.int32, (rows, 1), 0) & (tok_rows - 1)
    )
    lane = lax.broadcasted_iota(jnp.int32, (1, chunk_keys), 1)
    lane_block = lax.shift_right_logical(lane, shift)
    lane_row = lane & (tok_rows - 1)

    def chunk_keys_of(c, g):
        k = kv_ref[c * chunk_blocks : (c + 1) * chunk_blocks, g * tok_rows : (g + 1) * tok_rows, :]
        return k.reshape(chunk_keys, head_width)

    def chunk_values_of(c, g):
        base = kv_heads * tok_rows + g * tok_rows
        v = kv_ref[c * chunk_blocks : (c + 1) * chunk_blocks, base : base + tok_rows, :]
        return v.reshape(chunk_keys, head_width)

    def chunk_scores(q, k, c):
        s = lax.dot_general(q, k, (((1,), (1,)), ((), ())), preferred_element_type=f32) * scale
        key_off = jnp.zeros((1, chunk_keys), jnp.int32)
        for b in range(chunk_blocks):
            key_off = jnp.where(lane_block == b, offs_ref[c * chunk_blocks + b], key_off)
        visible = (key_off * tok_rows + lane_row) <= row_pos
        return jnp.where(visible, s, MASKED), visible

    for g in range(kv_heads):
        heads = slice(g * heads_per_group, (g + 1) * heads_per_group)
        q = q_ref[heads].reshape(rows, head_width)
        do = do_ref[heads].reshape(rows, head_width)
        fo = fo_ref[heads].reshape(rows, head_width)
        delta = jnp.sum(do.astype(f32) * fo.astype(f32), axis=1, keepdims=True)

        run_max = jnp.full((rows, 1), MASKED, f32)
        run_total = jnp.zeros((rows, 1), f32)
        single = blocks == chunk_blocks
        for c in range(blocks // chunk_blocks):
            s, visible = chunk_scores(q, chunk_keys_of(c, g), c)
            new_max = jnp.maximum(run_max, jnp.max(s, axis=1, keepdims=True))
            lifted = jnp.exp(s - new_max)
            run_total = run_total * jnp.exp(run_max - new_max) + jnp.sum(
                lifted, axis=1, keepdims=True
            )
            run_max = new_max
        log_total = run_max + jnp.log(run_total)

        dq = jnp.zeros((rows, head_width), f32)
        for c in range(blocks // chunk_blocks):
            k = chunk_keys_of(c, g)
            v = chunk_values_of(c, g)
            if single:
                probs = lifted * (1.0 / run_total)
            else:
                s, visible = chunk_scores(q, k, c)
                probs = jnp.exp(s - log_total)
            prob_grad = lax.dot_general(
                do, v, (((1,), (1,)), ((), ())), preferred_element_type=f32
            )
            score_grad = (probs * (prob_grad - delta)).astype(jnp.bfloat16)
            dq = dq + jnp.dot(score_grad, k, preferred_element_type=f32)
            dk = scale * lax.dot_general(
                q, score_grad, (((0,), (0,)), ((), ())), preferred_element_type=f32
            ).T
            dv = lax.dot_general(
                do, probs.astype(jnp.bfloat16), (((0,), (0,)), ((), ())), preferred_element_type=f32
            ).T
            for b in range(chunk_blocks):
                block = c * chunk_blocks + b
                piece = slice(b * tok_rows, (b + 1) * tok_rows)
                if block == 0:
                    own_part_ref[g] = dk[piece]
                    own_part_ref[kv_heads + g] = dv[piece]
                else:
                    parts_ref[block - 1, g] = dk[piece].astype(jnp.bfloat16)
                    parts_ref[block - 1, kv_heads + g] = dv[piece].astype(jnp.bfloat16)
                if block == blocks // 2:
                    mirror_part_ref[g] = dk[piece]
                    mirror_part_ref[kv_heads + g] = dv[piece]
        dq_ref[heads] = (scale * dq).reshape(heads_per_group, tok_rows, head_width)


def local_backward(offsets, own_offset, q_t, do_t, fo_t, gathered, kv_heads):
    q_heads, tok_rows, head_width = q_t.shape
    blocks = gathered.shape[0]
    chunk_blocks = min(CHUNK_BLOCKS, blocks)
    rows = q_heads * tok_rows
    keys = blocks * tok_rows
    smem = pl.BlockSpec(memory_space=pltpu.SMEM)
    vmem = pl.BlockSpec(memory_space=pltpu.VMEM)
    return pl.pallas_call(
        functools.partial(backward_kernel, kv_heads=kv_heads, chunk_blocks=chunk_blocks),
        out_shape=(
            jax.ShapeDtypeStruct((q_heads, tok_rows, head_width), jnp.float32),
            jax.ShapeDtypeStruct((2 * kv_heads, tok_rows, head_width), jnp.float32),
            jax.ShapeDtypeStruct((2 * kv_heads, tok_rows, head_width), jnp.float32),
            jax.ShapeDtypeStruct((blocks - 1, 2 * kv_heads, tok_rows, head_width), jnp.bfloat16),
        ),
        in_specs=[smem, smem, vmem, vmem, vmem, vmem],
        out_specs=(vmem, vmem, vmem, vmem),
        compiler_params=pltpu.CompilerParams(vmem_limit_bytes=48 * 1024 * 1024),
        cost_estimate=pl.CostEstimate(
            flops=12 * rows * keys * head_width,
            transcendentals=2 * rows * keys,
            bytes_accessed=gathered.size * 2 + 3 * q_t.size * 2 + 6 * q_t.size,
        ),
    )(offsets, own_offset, q_t, do_t, fo_t, gathered)


def on_device(query_vectors, key_vectors, value_rows, forward_out, out_grad, block_offsets):
    tok_rows, q_heads, head_width = query_vectors.shape
    kv_heads = key_vectors.shape[1]
    cycle_size = lax.axis_size("ctx")
    kv_rows = tok_rows * kv_heads

    offset_rows = jnp.full((OFFSET_ROWS, head_width), block_offsets[0], jnp.float32).astype(jnp.bfloat16)
    paired = jnp.concatenate([key_vectors, value_rows], axis=1).transpose(1, 0, 2)
    slab = jnp.concatenate([paired.reshape(2 * kv_rows, head_width), offset_rows], axis=0)
    half = cycle_size // 2
    from_mirror = lax.ppermute(slab, "ctx", mirror_pairs(cycle_size))
    if half == 4:
        from_x1 = lax.ppermute(slab, "ctx", mate_pairs(cycle_size, 1))
        from_x2 = lax.ppermute(slab, "ctx", mate_pairs(cycle_size, 2))
        pair = lax.ppermute(jnp.stack([from_mirror, from_x2]), "ctx", mate_pairs(cycle_size, 1))
        mirror_of_x2 = lax.ppermute(from_mirror, "ctx", mate_pairs(cycle_size, 2))
        mirror_of_x3 = lax.ppermute(from_mirror, "ctx", mate_pairs(cycle_size, 3))
        blocks = [slab, from_x1, from_x2, pair[1], from_mirror, pair[0], mirror_of_x2, mirror_of_x3]
    else:
        from_mates = [lax.ppermute(slab, "ctx", mate_pairs(cycle_size, k)) for k in range(1, half)]
        handed_on = [
            lax.ppermute(from_mirror, "ctx", mate_pairs(cycle_size, k)) for k in range(1, half)
        ]
        blocks = [slab] + from_mates + [from_mirror] + handed_on
    gathered = jnp.stack(blocks)
    all_offsets = gathered[:, 2 * kv_rows, 0].astype(jnp.float32).astype(jnp.int32)

    dq_t, own_part, mirror_part, parts = local_backward(
        all_offsets,
        block_offsets,
        query_vectors.transpose(1, 0, 2),
        out_grad.transpose(1, 0, 2),
        forward_out.transpose(1, 0, 2),
        gathered,
        kv_heads,
    )
    mirror_total = mirror_part
    for k in range(1, half):
        arrived = lax.ppermute(parts[half + k - 1], "ctx", mate_pairs(cycle_size, k))
        mirror_total = mirror_total + arrived.astype(jnp.float32)
    parts, mirror_total = lax.optimization_barrier((parts, mirror_total))
    crossed = lax.ppermute(mirror_total.astype(jnp.bfloat16), "ctx", mirror_pairs(cycle_size))
    own_total = own_part
    for k in range(1, half):
        arrived = lax.ppermute(parts[k - 1], "ctx", mate_pairs(cycle_size, k))
        own_total = own_total + arrived.astype(jnp.float32)
    total = own_total + crossed.astype(jnp.float32)
    key_grad = total[:kv_heads].transpose(1, 0, 2)
    value_grad = total[kv_heads:].transpose(1, 0, 2)
    return (dq_t.transpose(1, 0, 2), key_grad, value_grad)


def solution(mesh):
    in_specs = (
        P(("groups", "ctx"), "heads", None),
        P(("groups", "ctx"), "heads", None),
        P(("groups", "ctx"), "heads", None),
        P(("groups", "ctx"), "heads", None),
        P(("groups", "ctx"), "heads", None),
        P(("groups", "ctx")),
    )
    out_specs = (
        P(("groups", "ctx"), "heads", None),
        P(("groups", "ctx"), "heads", None),
        P(("groups", "ctx"), "heads", None),
    )
    return jax.shard_map(
        on_device, mesh=mesh, in_specs=in_specs, out_specs=out_specs, check_vma=False
    )
```

```python
import functools

import jax
import jax.numpy as jnp
from jax import lax
from jax.experimental import pallas as pl
from jax.experimental.pallas import tpu as pltpu
from jax.sharding import PartitionSpec as P

OFFSET_ROWS = 16
CHUNK_BLOCKS = 8
MASKED = -1e30


def mate_pairs(peers, by):
    half = peers // 2
    assert half & (half - 1) == 0
    return [(i, half * (i // half) + ((i % half) ^ by)) for i in range(peers)]


def mirror_pairs(peers):
    return [(i, (i + peers // 2) % peers) for i in range(peers)]


def backward_kernel(
    offs_ref, own_ref, q_ref, do_ref, fo_ref, kv_ref, dq_ref, own_part_ref, mirror_part_ref,
    parts_ref, *, kv_heads, chunk_blocks
):
    q_heads, tok_rows, head_width = q_ref.shape
    blocks = kv_ref.shape[0]
    heads_per_group = q_heads // kv_heads
    rows = heads_per_group * tok_rows
    chunk_keys = chunk_blocks * tok_rows
    shift = tok_rows.bit_length() - 1
    scale = head_width ** (-0.5)
    f32 = jnp.float32
    row_pos = own_ref[0] * tok_rows + (
        lax.broadcasted_iota(jnp.int32, (rows, 1), 0) & (tok_rows - 1)
    )
    lane = lax.broadcasted_iota(jnp.int32, (1, chunk_keys), 1)
    lane_block = lax.shift_right_logical(lane, shift)
    lane_row = lane & (tok_rows - 1)

    def chunk_keys_of(c, g):
        k = kv_ref[c * chunk_blocks : (c + 1) * chunk_blocks, g * tok_rows : (g + 1) * tok_rows, :]
        return k.reshape(chunk_keys, head_width)

    def chunk_values_of(c, g):
        base = kv_heads * tok_rows + g * tok_rows
        v = kv_ref[c * chunk_blocks : (c + 1) * chunk_blocks, base : base + tok_rows, :]
        return v.reshape(chunk_keys, head_width)

    def chunk_scores(q, k, c):
        s = lax.dot_general(q, k, (((1,), (1,)), ((), ())), preferred_element_type=f32) * scale
        key_off = jnp.zeros((1, chunk_keys), jnp.int32)
        for b in range(chunk_blocks):
            key_off = jnp.where(lane_block == b, offs_ref[c * chunk_blocks + b], key_off)
        visible = (key_off * tok_rows + lane_row) <= row_pos
        return jnp.where(visible, s, MASKED), visible

    for g in range(kv_heads):
        heads = slice(g * heads_per_group, (g + 1) * heads_per_group)
        q = q_ref[heads].reshape(rows, head_width)
        do = do_ref[heads].reshape(rows, head_width)
        fo = fo_ref[heads].reshape(rows, head_width)
        delta = jnp.sum(do.astype(f32) * fo.astype(f32), axis=1, keepdims=True)

        run_max = jnp.full((rows, 1), MASKED, f32)
        run_total = jnp.zeros((rows, 1), f32)
        single = blocks == chunk_blocks
        for c in range(blocks // chunk_blocks):
            s, visible = chunk_scores(q, chunk_keys_of(c, g), c)
            new_max = jnp.maximum(run_max, jnp.max(s, axis=1, keepdims=True))
            lifted = jnp.exp(s - new_max)
            run_total = run_total * jnp.exp(run_max - new_max) + jnp.sum(
                lifted, axis=1, keepdims=True
            )
            run_max = new_max
        log_total = run_max + jnp.log(run_total)

        dq = jnp.zeros((rows, head_width), f32)
        for c in range(blocks // chunk_blocks):
            k = chunk_keys_of(c, g)
            v = chunk_values_of(c, g)
            if single:
                probs = lifted * (1.0 / run_total)
            else:
                s, visible = chunk_scores(q, k, c)
                probs = jnp.exp(s - log_total)
            prob_grad = lax.dot_general(
                do, v, (((1,), (1,)), ((), ())), preferred_element_type=f32
            )
            score_grad = (probs * (prob_grad - delta)).astype(jnp.bfloat16)
            dq = dq + jnp.dot(score_grad, k, preferred_element_type=f32)
            dk = scale * lax.dot_general(
                q, score_grad, (((0,), (0,)), ((), ())), preferred_element_type=f32
            ).T
            dv = lax.dot_general(
                do, probs.astype(jnp.bfloat16), (((0,), (0,)), ((), ())), preferred_element_type=f32
            ).T
            for b in range(chunk_blocks):
                block = c * chunk_blocks + b
                piece = slice(b * tok_rows, (b + 1) * tok_rows)
                if block == 0:
                    own_part_ref[g] = dk[piece]
                    own_part_ref[kv_heads + g] = dv[piece]
                else:
                    parts_ref[block - 1, g] = dk[piece].astype(jnp.bfloat16)
                    parts_ref[block - 1, kv_heads + g] = dv[piece].astype(jnp.bfloat16)
                if block == blocks // 2:
                    mirror_part_ref[g] = dk[piece]
                    mirror_part_ref[kv_heads + g] = dv[piece]
        dq_ref[heads] = (scale * dq).reshape(heads_per_group, tok_rows, head_width)


def local_backward(offsets, own_offset, q_t, do_t, fo_t, gathered, kv_heads):
    q_heads, tok_rows, head_width = q_t.shape
    blocks = gathered.shape[0]
    chunk_blocks = min(CHUNK_BLOCKS, blocks)
    rows = q_heads * tok_rows
    keys = blocks * tok_rows
    smem = pl.BlockSpec(memory_space=pltpu.SMEM)
    vmem = pl.BlockSpec(memory_space=pltpu.VMEM)
    return pl.pallas_call(
        functools.partial(backward_kernel, kv_heads=kv_heads, chunk_blocks=chunk_blocks),
        out_shape=(
            jax.ShapeDtypeStruct((q_heads, tok_rows, head_width), jnp.float32),
            jax.ShapeDtypeStruct((2 * kv_heads, tok_rows, head_width), jnp.float32),
            jax.ShapeDtypeStruct((2 * kv_heads, tok_rows, head_width), jnp.float32),
            jax.ShapeDtypeStruct((blocks - 1, 2 * kv_heads, tok_rows, head_width), jnp.bfloat16),
        ),
        in_specs=[smem, smem, vmem, vmem, vmem, vmem],
        out_specs=(vmem, vmem, vmem, vmem),
        compiler_params=pltpu.CompilerParams(vmem_limit_bytes=48 * 1024 * 1024),
        cost_estimate=pl.CostEstimate(
            flops=12 * rows * keys * head_width,
            transcendentals=2 * rows * keys,
            bytes_accessed=gathered.size * 2 + 3 * q_t.size * 2 + 6 * q_t.size,
        ),
    )(offsets, own_offset, q_t, do_t, fo_t, gathered)


def on_device(query_vectors, key_vectors, value_rows, forward_out, out_grad, block_offsets):
    tok_rows, q_heads, head_width = query_vectors.shape
    kv_heads = key_vectors.shape[1]
    cycle_size = lax.axis_size("ctx")
    kv_rows = tok_rows * kv_heads

    offset_rows = jnp.full((OFFSET_ROWS, head_width), block_offsets[0], jnp.float32).astype(jnp.bfloat16)
    paired = jnp.concatenate([key_vectors, value_rows], axis=1).transpose(1, 0, 2)
    slab = jnp.concatenate([paired.reshape(2 * kv_rows, head_width), offset_rows], axis=0)
    half = cycle_size // 2
    from_mirror = lax.ppermute(slab, "ctx", mirror_pairs(cycle_size))
    if half == 4:
        from_x1 = lax.ppermute(slab, "ctx", mate_pairs(cycle_size, 1))
        from_x2 = lax.ppermute(slab, "ctx", mate_pairs(cycle_size, 2))
        from_x3 = lax.ppermute(from_x2, "ctx", mate_pairs(cycle_size, 1))
        mirror_of_x1 = lax.ppermute(from_mirror, "ctx", mate_pairs(cycle_size, 1))
        mirror_of_x2 = lax.ppermute(from_mirror, "ctx", mate_pairs(cycle_size, 2))
        mirror_of_x3 = lax.ppermute(from_mirror, "ctx", mate_pairs(cycle_size, 3))
        blocks = [slab, from_x1, from_x2, from_x3, from_mirror, mirror_of_x1, mirror_of_x2, mirror_of_x3]
    else:
        from_mates = [lax.ppermute(slab, "ctx", mate_pairs(cycle_size, k)) for k in range(1, half)]
        handed_on = [
            lax.ppermute(from_mirror, "ctx", mate_pairs(cycle_size, k)) for k in range(1, half)
        ]
        blocks = [slab] + from_mates + [from_mirror] + handed_on
    gathered = jnp.stack(blocks)
    all_offsets = gathered[:, 2 * kv_rows, 0].astype(jnp.float32).astype(jnp.int32)

    dq_t, own_part, mirror_part, parts = local_backward(
        all_offsets,
        block_offsets,
        query_vectors.transpose(1, 0, 2),
        out_grad.transpose(1, 0, 2),
        forward_out.transpose(1, 0, 2),
        gathered,
        kv_heads,
    )
    mirror_total = mirror_part
    for k in range(1, half):
        arrived = lax.ppermute(parts[half + k - 1], "ctx", mate_pairs(cycle_size, k))
        mirror_total = mirror_total + arrived.astype(jnp.float32)
    own_total = own_part
    for k in range(1, half):
        arrived = lax.ppermute(parts[k - 1], "ctx", mate_pairs(cycle_size, k))
        own_total = own_total + arrived.astype(jnp.float32)
    crossed = lax.ppermute(mirror_total.astype(jnp.bfloat16), "ctx", mirror_pairs(cycle_size))
    total = own_total + crossed.astype(jnp.float32)
    key_grad = total[:kv_heads].transpose(1, 0, 2)
    value_grad = total[kv_heads:].transpose(1, 0, 2)
    return (dq_t.transpose(1, 0, 2), key_grad, value_grad)


def solution(mesh):
    in_specs = (
        P(("groups", "ctx"), "heads", None),
        P(("groups", "ctx"), "heads", None),
        P(("groups", "ctx"), "heads", None),
        P(("groups", "ctx"), "heads", None),
        P(("groups", "ctx"), "heads", None),
        P(("groups", "ctx")),
    )
    out_specs = (
        P(("groups", "ctx"), "heads", None),
        P(("groups", "ctx"), "heads", None),
        P(("groups", "ctx"), "heads", None),
    )
    return jax.shard_map(
        on_device, mesh=mesh, in_specs=in_specs, out_specs=out_specs, check_vma=False
    )
```

```python
import functools

import jax
import jax.numpy as jnp
from jax import lax
from jax.experimental import pallas as pl
from jax.experimental.pallas import tpu as pltpu
from jax.sharding import PartitionSpec as P

OFFSET_ROWS = 16
CHUNK_BLOCKS = 8
MASKED = -1e30


def mate_pairs(peers, by):
    half = peers // 2
    assert half & (half - 1) == 0
    return [(i, half * (i // half) + ((i % half) ^ by)) for i in range(peers)]


def mirror_pairs(peers):
    return [(i, (i + peers // 2) % peers) for i in range(peers)]


def backward_kernel(
    offs_ref, own_ref, q_ref, do_ref, fo_ref, kv_ref, dq_ref, own_part_ref, mirror_part_ref,
    parts_ref, *, kv_heads, chunk_blocks
):
    q_heads, tok_rows, head_width = q_ref.shape
    blocks = kv_ref.shape[0]
    heads_per_group = q_heads // kv_heads
    rows = heads_per_group * tok_rows
    chunk_keys = chunk_blocks * tok_rows
    shift = tok_rows.bit_length() - 1
    scale = head_width ** (-0.5)
    f32 = jnp.float32
    row_pos = own_ref[0] * tok_rows + (
        lax.broadcasted_iota(jnp.int32, (rows, 1), 0) & (tok_rows - 1)
    )
    lane = lax.broadcasted_iota(jnp.int32, (1, chunk_keys), 1)
    lane_block = lax.shift_right_logical(lane, shift)
    lane_row = lane & (tok_rows - 1)

    def chunk_keys_of(c, g):
        k = kv_ref[c * chunk_blocks : (c + 1) * chunk_blocks, g * tok_rows : (g + 1) * tok_rows, :]
        return k.reshape(chunk_keys, head_width)

    def chunk_values_of(c, g):
        base = kv_heads * tok_rows + g * tok_rows
        v = kv_ref[c * chunk_blocks : (c + 1) * chunk_blocks, base : base + tok_rows, :]
        return v.reshape(chunk_keys, head_width)

    def chunk_visible(c):
        key_off = jnp.zeros((1, chunk_keys), jnp.int32)
        for b in range(chunk_blocks):
            key_off = jnp.where(lane_block == b, offs_ref[c * chunk_blocks + b], key_off)
        return (key_off * tok_rows + lane_row) <= row_pos

    visibles = [chunk_visible(c) for c in range(blocks // chunk_blocks)]

    def chunk_scores(q, k, c):
        s = lax.dot_general(q, k, (((1,), (1,)), ((), ())), preferred_element_type=f32) * scale
        visible = visibles[c]
        return jnp.where(visible, s, MASKED), visible

    for g in range(kv_heads):
        heads = slice(g * heads_per_group, (g + 1) * heads_per_group)
        q = q_ref[heads].reshape(rows, head_width)
        do = do_ref[heads].reshape(rows, head_width)
        fo = fo_ref[heads].reshape(rows, head_width)
        delta = jnp.sum(do.astype(f32) * fo.astype(f32), axis=1, keepdims=True)

        run_max = jnp.full((rows, 1), MASKED, f32)
        run_total = jnp.zeros((rows, 1), f32)
        single = blocks == chunk_blocks
        for c in range(blocks // chunk_blocks):
            s, visible = chunk_scores(q, chunk_keys_of(c, g), c)
            new_max = jnp.maximum(run_max, jnp.max(s, axis=1, keepdims=True))
            lifted = jnp.exp(s - new_max)
            run_total = run_total * jnp.exp(run_max - new_max) + jnp.sum(
                lifted, axis=1, keepdims=True
            )
            run_max = new_max
        log_total = run_max + jnp.log(run_total)

        dq = jnp.zeros((rows, head_width), f32)
        for c in range(blocks // chunk_blocks):
            k = chunk_keys_of(c, g)
            v = chunk_values_of(c, g)
            if single:
                probs = lifted * (1.0 / run_total)
            else:
                s, visible = chunk_scores(q, k, c)
                probs = jnp.exp(s - log_total)
            prob_grad = lax.dot_general(
                do, v, (((1,), (1,)), ((), ())), preferred_element_type=f32
            )
            score_grad = (probs * (prob_grad - delta)).astype(jnp.bfloat16)
            dq = dq + jnp.dot(score_grad, k, preferred_element_type=f32)
            dk = scale * lax.dot_general(
                q, score_grad, (((0,), (0,)), ((), ())), preferred_element_type=f32
            ).T
            dv = lax.dot_general(
                do, probs.astype(jnp.bfloat16), (((0,), (0,)), ((), ())), preferred_element_type=f32
            ).T
            for b in range(chunk_blocks):
                block = c * chunk_blocks + b
                piece = slice(b * tok_rows, (b + 1) * tok_rows)
                if block == 0:
                    own_part_ref[g] = dk[piece]
                    own_part_ref[kv_heads + g] = dv[piece]
                else:
                    parts_ref[block - 1, g] = dk[piece].astype(jnp.bfloat16)
                    parts_ref[block - 1, kv_heads + g] = dv[piece].astype(jnp.bfloat16)
                if block == blocks // 2:
                    mirror_part_ref[g] = dk[piece]
                    mirror_part_ref[kv_heads + g] = dv[piece]
        dq_ref[heads] = (scale * dq).reshape(heads_per_group, tok_rows, head_width)


def local_backward(offsets, own_offset, q_t, do_t, fo_t, gathered, kv_heads):
    q_heads, tok_rows, head_width = q_t.shape
    blocks = gathered.shape[0]
    chunk_blocks = min(CHUNK_BLOCKS, blocks)
    rows = q_heads * tok_rows
    keys = blocks * tok_rows
    smem = pl.BlockSpec(memory_space=pltpu.SMEM)
    vmem = pl.BlockSpec(memory_space=pltpu.VMEM)
    return pl.pallas_call(
        functools.partial(backward_kernel, kv_heads=kv_heads, chunk_blocks=chunk_blocks),
        out_shape=(
            jax.ShapeDtypeStruct((q_heads, tok_rows, head_width), jnp.float32),
            jax.ShapeDtypeStruct((2 * kv_heads, tok_rows, head_width), jnp.float32),
            jax.ShapeDtypeStruct((2 * kv_heads, tok_rows, head_width), jnp.float32),
            jax.ShapeDtypeStruct((blocks - 1, 2 * kv_heads, tok_rows, head_width), jnp.bfloat16),
        ),
        in_specs=[smem, smem, vmem, vmem, vmem, vmem],
        out_specs=(vmem, vmem, vmem, vmem),
        compiler_params=pltpu.CompilerParams(vmem_limit_bytes=48 * 1024 * 1024),
        cost_estimate=pl.CostEstimate(
            flops=12 * rows * keys * head_width,
            transcendentals=2 * rows * keys,
            bytes_accessed=gathered.size * 2 + 3 * q_t.size * 2 + 6 * q_t.size,
        ),
    )(offsets, own_offset, q_t, do_t, fo_t, gathered)


def on_device(query_vectors, key_vectors, value_rows, forward_out, out_grad, block_offsets):
    tok_rows, q_heads, head_width = query_vectors.shape
    kv_heads = key_vectors.shape[1]
    cycle_size = lax.axis_size("ctx")
    kv_rows = tok_rows * kv_heads

    offset_rows = jnp.full((OFFSET_ROWS, head_width), block_offsets[0], jnp.float32).astype(jnp.bfloat16)
    paired = jnp.concatenate([key_vectors, value_rows], axis=1).transpose(1, 0, 2)
    slab = jnp.concatenate([paired.reshape(2 * kv_rows, head_width), offset_rows], axis=0)
    half = cycle_size // 2
    from_mirror = lax.ppermute(slab, "ctx", mirror_pairs(cycle_size))
    if half == 4:
        from_x1 = lax.ppermute(slab, "ctx", mate_pairs(cycle_size, 1))
        from_x2 = lax.ppermute(slab, "ctx", mate_pairs(cycle_size, 2))
        from_x3 = lax.ppermute(from_x2, "ctx", mate_pairs(cycle_size, 1))
        mirror_of_x1 = lax.ppermute(from_mirror, "ctx", mate_pairs(cycle_size, 1))
        mirror_of_x2 = lax.ppermute(from_mirror, "ctx", mate_pairs(cycle_size, 2))
        mirror_of_x3 = lax.ppermute(from_mirror, "ctx", mate_pairs(cycle_size, 3))
        blocks = [slab, from_x1, from_x2, from_x3, from_mirror, mirror_of_x1, mirror_of_x2, mirror_of_x3]
    else:
        from_mates = [lax.ppermute(slab, "ctx", mate_pairs(cycle_size, k)) for k in range(1, half)]
        handed_on = [
            lax.ppermute(from_mirror, "ctx", mate_pairs(cycle_size, k)) for k in range(1, half)
        ]
        blocks = [slab] + from_mates + [from_mirror] + handed_on
    gathered = jnp.stack(blocks)
    all_offsets = gathered[:, 2 * kv_rows, 0].astype(jnp.float32).astype(jnp.int32)

    dq_t, own_part, mirror_part, parts = local_backward(
        all_offsets,
        block_offsets,
        query_vectors.transpose(1, 0, 2),
        out_grad.transpose(1, 0, 2),
        forward_out.transpose(1, 0, 2),
        gathered,
        kv_heads,
    )
    mirror_total = mirror_part
    for k in range(1, half):
        arrived = lax.ppermute(parts[half + k - 1], "ctx", mate_pairs(cycle_size, k))
        mirror_total = mirror_total + arrived.astype(jnp.float32)
    own_total = own_part
    for k in range(1, half):
        arrived = lax.ppermute(parts[k - 1], "ctx", mate_pairs(cycle_size, k))
        own_total = own_total + arrived.astype(jnp.float32)
    crossed = lax.ppermute(mirror_total.astype(jnp.bfloat16), "ctx", mirror_pairs(cycle_size))
    total = own_total + crossed.astype(jnp.float32)
    key_grad = total[:kv_heads].transpose(1, 0, 2)
    value_grad = total[kv_heads:].transpose(1, 0, 2)
    return (dq_t.transpose(1, 0, 2), key_grad, value_grad)


def solution(mesh):
    in_specs = (
        P(("groups", "ctx"), "heads", None),
        P(("groups", "ctx"), "heads", None),
        P(("groups", "ctx"), "heads", None),
        P(("groups", "ctx"), "heads", None),
        P(("groups", "ctx"), "heads", None),
        P(("groups", "ctx")),
    )
    out_specs = (
        P(("groups", "ctx"), "heads", None),
        P(("groups", "ctx"), "heads", None),
        P(("groups", "ctx"), "heads", None),
    )
    return jax.shard_map(
        on_device, mesh=mesh, in_specs=in_specs, out_specs=out_specs, check_vma=False
    )
```

```python
import functools

import jax
import jax.numpy as jnp
from jax import lax
from jax.experimental import pallas as pl
from jax.experimental.pallas import tpu as pltpu
from jax.sharding import PartitionSpec as P

OFFSET_ROWS = 16
CHUNK_BLOCKS = 8
MASKED = -1e30


def mate_pairs(peers, by):
    half = peers // 2
    assert half & (half - 1) == 0
    return [(i, half * (i // half) + ((i % half) ^ by)) for i in range(peers)]


def mirror_pairs(peers):
    return [(i, (i + peers // 2) % peers) for i in range(peers)]


def backward_kernel(
    offs_ref, own_ref, q_ref, do_ref, fo_ref, kv_ref, dq_ref, own_part_ref, mirror_part_ref,
    parts_ref, *, kv_heads, chunk_blocks
):
    q_heads, tok_rows, head_width = q_ref.shape
    blocks = kv_ref.shape[0]
    heads_per_group = q_heads // kv_heads
    rows = heads_per_group * tok_rows
    chunk_keys = chunk_blocks * tok_rows
    shift = tok_rows.bit_length() - 1
    scale = head_width ** (-0.5)
    f32 = jnp.float32
    row_pos = own_ref[0] * tok_rows + (
        lax.broadcasted_iota(jnp.int32, (rows, 1), 0) & (tok_rows - 1)
    )
    lane = lax.broadcasted_iota(jnp.int32, (1, chunk_keys), 1)
    lane_block = lax.shift_right_logical(lane, shift)
    lane_row = lane & (tok_rows - 1)

    def chunk_keys_of(c, g):
        k = kv_ref[c * chunk_blocks : (c + 1) * chunk_blocks, g * tok_rows : (g + 1) * tok_rows, :]
        return k.reshape(chunk_keys, head_width)

    def chunk_values_of(c, g):
        base = kv_heads * tok_rows + g * tok_rows
        v = kv_ref[c * chunk_blocks : (c + 1) * chunk_blocks, base : base + tok_rows, :]
        return v.reshape(chunk_keys, head_width)

    def chunk_scores(q, k, c):
        s = lax.dot_general(q, k, (((1,), (1,)), ((), ())), preferred_element_type=f32) * scale
        key_off = jnp.zeros((1, chunk_keys), jnp.int32)
        for b in range(chunk_blocks):
            key_off = jnp.where(lane_block == b, offs_ref[c * chunk_blocks + b], key_off)
        visible = (key_off * tok_rows + lane_row) <= row_pos
        return jnp.where(visible, s, MASKED), visible

    for g in range(kv_heads):
        heads = slice(g * heads_per_group, (g + 1) * heads_per_group)
        q = q_ref[heads].reshape(rows, head_width)
        do = do_ref[heads].reshape(rows, head_width)
        fo = fo_ref[heads].reshape(rows, head_width)
        delta = jnp.sum(do.astype(f32) * fo.astype(f32), axis=1, keepdims=True)

        run_max = jnp.full((rows, 1), MASKED, f32)
        run_total = jnp.zeros((rows, 1), f32)
        single = blocks == chunk_blocks
        for c in range(blocks // chunk_blocks):
            s, visible = chunk_scores(q, chunk_keys_of(c, g), c)
            new_max = jnp.maximum(run_max, jnp.max(s, axis=1, keepdims=True))
            lifted = jnp.exp(s - new_max)
            run_total = run_total * jnp.exp(run_max - new_max) + jnp.sum(
                lifted, axis=1, keepdims=True
            )
            run_max = new_max
        log_total = run_max + jnp.log(run_total)

        dq = jnp.zeros((rows, head_width), f32)
        for c in range(blocks // chunk_blocks):
            k = chunk_keys_of(c, g)
            v = chunk_values_of(c, g)
            if single:
                probs = lifted * (1.0 / run_total)
            else:
                s, visible = chunk_scores(q, k, c)
                probs = jnp.exp(s - log_total)
            prob_grad = lax.dot_general(
                do, v, (((1,), (1,)), ((), ())), preferred_element_type=f32
            )
            score_grad = (probs * (prob_grad - delta)).astype(jnp.bfloat16)
            dq = dq + jnp.dot(score_grad, k, preferred_element_type=f32)
            dk = scale * lax.dot_general(
                q, score_grad, (((0,), (0,)), ((), ())), preferred_element_type=f32
            ).T
            dv = lax.dot_general(
                do, probs.astype(jnp.bfloat16), (((0,), (0,)), ((), ())), preferred_element_type=f32
            ).T
            for b in range(chunk_blocks):
                block = c * chunk_blocks + b
                piece = slice(b * tok_rows, (b + 1) * tok_rows)
                if block == 0:
                    own_part_ref[g] = dk[piece]
                    own_part_ref[kv_heads + g] = dv[piece]
                else:
                    parts_ref[block - 1, g] = dk[piece].astype(jnp.bfloat16)
                    parts_ref[block - 1, kv_heads + g] = dv[piece].astype(jnp.bfloat16)
                if block == blocks // 2:
                    mirror_part_ref[g] = dk[piece]
                    mirror_part_ref[kv_heads + g] = dv[piece]
        dq_ref[heads] = (scale * dq).reshape(heads_per_group, tok_rows, head_width)


def local_backward(offsets, own_offset, q_t, do_t, fo_t, gathered, kv_heads):
    q_heads, tok_rows, head_width = q_t.shape
    blocks = gathered.shape[0]
    chunk_blocks = min(CHUNK_BLOCKS, blocks)
    rows = q_heads * tok_rows
    keys = blocks * tok_rows
    smem = pl.BlockSpec(memory_space=pltpu.SMEM)
    vmem = pl.BlockSpec(memory_space=pltpu.VMEM)
    return pl.pallas_call(
        functools.partial(backward_kernel, kv_heads=kv_heads, chunk_blocks=chunk_blocks),
        out_shape=(
            jax.ShapeDtypeStruct((q_heads, tok_rows, head_width), jnp.float32),
            jax.ShapeDtypeStruct((2 * kv_heads, tok_rows, head_width), jnp.float32),
            jax.ShapeDtypeStruct((2 * kv_heads, tok_rows, head_width), jnp.float32),
            jax.ShapeDtypeStruct((blocks - 1, 2 * kv_heads, tok_rows, head_width), jnp.bfloat16),
        ),
        in_specs=[smem, smem, vmem, vmem, vmem, vmem],
        out_specs=(vmem, vmem, vmem, vmem),
        compiler_params=pltpu.CompilerParams(vmem_limit_bytes=48 * 1024 * 1024),
        cost_estimate=pl.CostEstimate(
            flops=12 * rows * keys * head_width,
            transcendentals=2 * rows * keys,
            bytes_accessed=gathered.size * 2 + 3 * q_t.size * 2 + 6 * q_t.size,
        ),
    )(offsets, own_offset, q_t, do_t, fo_t, gathered)


def on_device(query_vectors, key_vectors, value_rows, forward_out, out_grad, block_offsets):
    tok_rows, q_heads, head_width = query_vectors.shape
    kv_heads = key_vectors.shape[1]
    cycle_size = lax.axis_size("ctx")
    kv_rows = tok_rows * kv_heads

    offset_rows = jnp.full((OFFSET_ROWS, head_width), block_offsets[0], jnp.float32).astype(jnp.bfloat16)
    paired = jnp.concatenate([key_vectors, value_rows], axis=1).transpose(1, 0, 2)
    slab = jnp.concatenate([paired.reshape(2 * kv_rows, head_width), offset_rows], axis=0)
    half = cycle_size // 2
    from_mirror = lax.ppermute(slab, "ctx", mirror_pairs(cycle_size))
    if half == 4:
        from_x1 = lax.ppermute(slab, "ctx", mate_pairs(cycle_size, 1))
        from_x2 = lax.ppermute(slab, "ctx", mate_pairs(cycle_size, 2))
        from_x3 = lax.ppermute(from_x2, "ctx", mate_pairs(cycle_size, 1))
        mirror_of_x1 = lax.ppermute(from_mirror, "ctx", mate_pairs(cycle_size, 1))
        mirror_of_x2 = lax.ppermute(from_mirror, "ctx", mate_pairs(cycle_size, 2))
        mirror_of_x3 = lax.ppermute(from_mirror, "ctx", mate_pairs(cycle_size, 3))
        blocks = [slab, from_x1, from_x2, from_x3, from_mirror, mirror_of_x1, mirror_of_x2, mirror_of_x3]
    else:
        from_mates = [lax.ppermute(slab, "ctx", mate_pairs(cycle_size, k)) for k in range(1, half)]
        handed_on = [
            lax.ppermute(from_mirror, "ctx", mate_pairs(cycle_size, k)) for k in range(1, half)
        ]
        blocks = [slab] + from_mates + [from_mirror] + handed_on
    gathered = jnp.stack(blocks)
    all_offsets = gathered[:, 2 * kv_rows, 0].astype(jnp.float32).astype(jnp.int32)

    dq_t, own_part, mirror_part, parts = local_backward(
        all_offsets,
        block_offsets,
        query_vectors.transpose(1, 0, 2),
        out_grad.transpose(1, 0, 2),
        forward_out.transpose(1, 0, 2),
        gathered,
        kv_heads,
    )
    mirror_total = mirror_part
    for k in range(1, half):
        arrived = lax.ppermute(parts[half + k - 1], "ctx", mate_pairs(cycle_size, k))
        mirror_total = mirror_total + arrived.astype(jnp.float32)
    crossed = lax.ppermute(mirror_total.astype(jnp.bfloat16), "ctx", mirror_pairs(cycle_size))
    parts, crossed = lax.optimization_barrier((parts, crossed))
    own_total = own_part
    for k in range(1, half):
        arrived = lax.ppermute(parts[k - 1], "ctx", mate_pairs(cycle_size, k))
        own_total = own_total + arrived.astype(jnp.float32)
    total = own_total + crossed.astype(jnp.float32)
    key_grad = total[:kv_heads].transpose(1, 0, 2)
    value_grad = total[kv_heads:].transpose(1, 0, 2)
    return (dq_t.transpose(1, 0, 2), key_grad, value_grad)


def solution(mesh):
    in_specs = (
        P(("groups", "ctx"), "heads", None),
        P(("groups", "ctx"), "heads", None),
        P(("groups", "ctx"), "heads", None),
        P(("groups", "ctx"), "heads", None),
        P(("groups", "ctx"), "heads", None),
        P(("groups", "ctx")),
    )
    out_specs = (
        P(("groups", "ctx"), "heads", None),
        P(("groups", "ctx"), "heads", None),
        P(("groups", "ctx"), "heads", None),
    )
    return jax.shard_map(
        on_device, mesh=mesh, in_specs=in_specs, out_specs=out_specs, check_vma=False
    )
```
